512 devices in a mesh: role: 4 (over x), dp: 16 (over y, core), tp: 8 (over z).
Axes of the slice: x: 4, y: 8, z: 8, core: 2. Of those that a mesh axis runs over, the one named last changes fastest.
Arguments:
- states: bfloat16 [64, 10, 8192], P(('role', 'dp'), None, 'tp'), may hold values from -6 to 6
- lengths: int32 [64], replicated, may hold values from 1 to 10, 480 in all
- old_log_prob: float32 [64, 10], replicated, may hold values from -1.6 to -0.2
- up_weight: bfloat16 [4, 8192, 14336], P('role', 'tp', 'dp'), may hold values from -0.0625 to 0.0625
- down_weight: bfloat16 [4, 14336, 8192], P('role', 'dp', 'tp'), may hold values from -0.046875 to 0.046875
- score_head: float32 [4, 8192], P('role', 'tp'), may hold values from -0.0625 to 0.0625
Outputs:
- advantages: float32 [64, 10], replicated
- d_states: bfloat16 [64, 10, 8192], P(('role', 'dp'), None, 'tp')
The draws below stay inside these ranges and needn't reach their ends.
Inputs may be any that keep to these rules, and one draw needn't show every extreme that they name: The longest row is exactly 10 positions long, and the lengths sum to exactly 480.
All inputs are finite; a program needn't handle non-finite values.
Results may differ from the reference program's by a relative error of at most 0.024.
Values may be sent and summed in bfloat16 or wider, within the bound.
No kernel may reach another device: no remote copies, remote signals or barrier semaphores. Data moves between devices by JAX's collectives and lax.ppermute only.
A program may use at most 64 MiB of HBM per device.

```python
import math
import jax
import jax.numpy as jnp
import numpy as np
from jax import lax

D = 8192
HID = 14336
LEN = 10
ROWS = 64
LIVE = 480
N_ROLE = 4
N_TP = 8


def shard_levels(stream_key, shape, shards, smallest, high):
    gain, own = 1.0, jax.random.fold_in(stream_key, 6)
    for axis_at, shards_of in shards:
        steps = jnp.exp(jax.random.uniform(jax.random.fold_in(own, axis_at), (shards_of,), jnp.float32, smallest / len(shards), high / len(shards)))
        gain = gain * jnp.repeat(steps, shape[axis_at] // shards_of).reshape([-1 if axis == axis_at else 1 for axis in range(len(shape))])
    return gain


def split_up(number_of, total, reach, skew):
    loads = [(1 << 20) // math.isqrt(grade ** skew) + 1 for grade in range(2, number_of + 1)]
    rest, counts = total - reach - (number_of - 1), [1] * (number_of - 1)
    while rest > 0:
        candidates = [i for i in range(number_of - 1) if counts[i] < reach]
        mass, left = sum([loads[i] for i in candidates]), rest
        for i in candidates:
            addition = min(reach - counts[i], max(1, left * loads[i] // mass), rest)
            counts[i] = counts[i] + addition
            rest = rest - addition
    return np.array([reach] + counts)


def uneven_parts(stream_key, amount, total, most, slope):
    if amount == 2:
        one = jax.random.randint(stream_key, (), max(1, total - most), min(most, total - 1) + 1)
        return jnp.stack([one, total - one])
    sizes = jnp.asarray(split_up(amount, total, most, slope), jnp.int32)
    twos = (amount - 1) // 2
    source_of, receiver = sizes[1:1 + 2 * twos:2], sizes[2:2 + 2 * twos:2]
    room = jnp.minimum(source_of - 1, most - receiver)
    shifted = jax.random.randint(jax.random.fold_in(stream_key, 1), (twos,), 0, 1 << 20) % (room + 1)
    sizes = sizes.at[1:1 + 2 * twos:2].set(source_of - shifted).at[2:2 + 2 * twos:2].set(receiver + shifted)
    return sizes[jax.random.permutation(jax.random.fold_in(stream_key, 2), amount)]


def normal_values(stream_key, extent, scale, bound, split=(), kind=jnp.bfloat16):
    factor_of = shard_levels(stream_key, extent, split, -0.22, 0.18) if split else 1.0
    result = jax.random.normal(stream_key, extent, jnp.float32) * scale * factor_of
    return jnp.minimum(jnp.maximum(result, -bound), bound).astype(kind)


def setup_inputs(seed: int = 0) -> dict:
    seeds = jax.random.split(jax.random.key(seed), 7)
    states = normal_values(seeds[0], (ROWS, LEN, D), 1.0, 6.0, ((0, 64), (2, 8)))
    lengths = uneven_parts(seeds[1], ROWS, LIVE, LEN, 1).astype(jnp.int32)
    old_log_prob = jnp.clip(jax.random.uniform(seeds[2], (ROWS, LEN), jnp.float32, -1.6, -0.2), -1.6, -0.2)
    up_weight = normal_values(seeds[3], (N_ROLE, D, HID), D ** -0.5, 0.0625, ((0, 4), (1, 8), (2, 16)))
    down_weight = normal_values(seeds[4], (N_ROLE, HID, D), HID ** -0.5, 0.046875, ((0, 4), (1, 16), (2, 8)))
    score_head = normal_values(seeds[5], (N_ROLE, D), D ** -0.5, 0.0625, ((0, 4), (1, 8)), jnp.float32)
    return {"states": states, "lengths": lengths, "old_log_prob": old_log_prob, "up_weight": up_weight, "down_weight": down_weight, "score_head": score_head}


penalty_beta = 0.05
trace_lambda = 0.95
value_weight = 0.5
kl_weight = 0.1
loss_scale = 64.0

def decay_table(seq_len):
    positions = jnp.arange(seq_len, dtype=jnp.int32)
    steps_ahead = positions[None, :] - positions[:, None]
    weights = jnp.power(jnp.float32(trace_lambda), jnp.maximum(steps_ahead, 0).astype(jnp.float32))
    return jnp.where(steps_ahead >= 0, weights, jnp.float32(0.0))

def objective(scores, lengths, old_log_prob):
    row_count, seq_len = old_log_prob.shape
    positions = jnp.arange(seq_len, dtype=jnp.int32)
    live_mask = (positions[None, :] < lengths[:, None]).astype(jnp.float32)
    final_pos = (positions[None, :] == lengths[:, None] - 1).astype(jnp.float32)
    score_grid = scores.reshape(scores.shape[0], row_count, seq_len)
    log_prob = jax.nn.log_sigmoid(score_grid[0])
    ref_log_prob = jax.nn.log_sigmoid(score_grid[1])
    value_est = score_grid[3]
    outcome = lax.optimization_barrier(jnp.sum(score_grid[2] * final_pos, axis=1, keepdims=True))
    token_gain = live_mask * -penalty_beta * (log_prob - ref_log_prob) + final_pos * outcome
    frozen = live_mask * value_est
    next_value = jnp.concatenate([frozen[:, 1:], jnp.zeros((row_count, 1), jnp.float32)], axis=1)
    step_error = lax.stop_gradient(token_gain + next_value - frozen)
    advantage = live_mask * jnp.dot(step_error, decay_table(seq_len).T, precision=lax.Precision.HIGHEST)
    prob_ratio = jnp.exp(log_prob - old_log_prob)
    target = advantage + lax.stop_gradient(value_est)
    spread = ref_log_prob - log_prob
    per_token = -prob_ratio * advantage + value_weight * 0.5 * (value_est - target) ** 2 + kl_weight * (jnp.exp(spread) - spread - 1.0)
    return (loss_scale * jnp.sum(live_mask * per_token), advantage)

def silu_slope(preact):
    sigmoid_value = jax.nn.sigmoid(preact)
    return sigmoid_value * (1.0 + preact * (1.0 - sigmoid_value))

def reference(states, lengths, old_log_prob, up_weight, down_weight, score_head):
    row_count, seq_len, feature_width = states.shape
    tokens = states.reshape(-1, feature_width)
    part_width = feature_width // N_TP
    preacts = []
    scores = []
    for which_model in range(N_ROLE):
        preact = jnp.zeros((tokens.shape[0], up_weight.shape[2]), jnp.float32)
        for feature_block in range(N_TP):
            lower = feature_block * part_width
            partial_block = jnp.dot(tokens[:, lower:lower + part_width], up_weight[which_model, lower:lower + part_width], preferred_element_type=jnp.float32)
            preact = preact + lax.optimization_barrier(partial_block.astype(jnp.bfloat16)).astype(jnp.float32)
        activation = jax.nn.silu(preact).astype(jnp.bfloat16)
        branch = jnp.dot(activation, down_weight[which_model], preferred_element_type=jnp.float32)
        scores.append(lax.optimization_barrier(jnp.sum((tokens.astype(jnp.float32) + branch) * score_head[which_model], axis=1)))
        preacts.append(preact)
    slopes, advantage = jax.grad(objective, has_aux=True)(jnp.stack(scores), lengths, old_log_prob)
    grad_total = jnp.zeros(tokens.shape, jnp.float32)
    for which_model in range(N_ROLE):
        upstream = (slopes[which_model][:, None] * score_head[which_model][None, :]).astype(jnp.bfloat16)
        backflow = jnp.zeros(preacts[which_model].shape, jnp.float32)
        for feature_block in range(N_TP):
            lower = feature_block * part_width
            partial_block = jnp.dot(upstream[:, lower:lower + part_width], down_weight[which_model][:, lower:lower + part_width].T, preferred_element_type=jnp.float32)
            backflow = backflow + lax.optimization_barrier(partial_block.astype(jnp.bfloat16)).astype(jnp.float32)
        grad_pre = (backflow * silu_slope(preacts[which_model])).astype(jnp.bfloat16)
        grad_total = grad_total + upstream.astype(jnp.float32) + jnp.dot(grad_pre, up_weight[which_model].T, preferred_element_type=jnp.float32)
    return (advantage, grad_total.astype(jnp.bfloat16).reshape(row_count, seq_len, feature_width))
```

```python
import jax
import jax.numpy as jnp
from jax import lax
from jax.sharding import PartitionSpec as P

penalty_beta = 0.05
trace_lambda = 0.95
value_weight = 0.5
kl_weight = 0.1
loss_scale = 64.0


def decay_table(seq_len):
    positions = jnp.arange(seq_len, dtype=jnp.int32)
    steps_ahead = positions[None, :] - positions[:, None]
    weights = jnp.power(jnp.float32(trace_lambda), jnp.maximum(steps_ahead, 0).astype(jnp.float32))
    return jnp.where(steps_ahead >= 0, weights, jnp.float32(0.0))


def objective(scores, lengths, old_log_prob):
    row_count, seq_len = old_log_prob.shape
    positions = jnp.arange(seq_len, dtype=jnp.int32)
    live_mask = (positions[None, :] < lengths[:, None]).astype(jnp.float32)
    final_pos = (positions[None, :] == lengths[:, None] - 1).astype(jnp.float32)
    score_grid = scores.reshape(scores.shape[0], row_count, seq_len)
    log_prob = jax.nn.log_sigmoid(score_grid[0])
    ref_log_prob = jax.nn.log_sigmoid(score_grid[1])
    value_est = score_grid[3]
    outcome = jnp.sum(score_grid[2] * final_pos, axis=1, keepdims=True)
    token_gain = live_mask * -penalty_beta * (log_prob - ref_log_prob) + final_pos * outcome
    frozen = live_mask * value_est
    next_value = jnp.concatenate([frozen[:, 1:], jnp.zeros((row_count, 1), jnp.float32)], axis=1)
    step_error = lax.stop_gradient(token_gain + next_value - frozen)
    advantage = live_mask * jnp.dot(
        step_error, decay_table(seq_len).T, precision=lax.Precision.HIGHEST
    )
    prob_ratio = jnp.exp(log_prob - old_log_prob)
    target = advantage + lax.stop_gradient(value_est)
    spread = ref_log_prob - log_prob
    per_token = (
        -prob_ratio * advantage
        + value_weight * 0.5 * (value_est - target) ** 2
        + kl_weight * (jnp.exp(spread) - spread - 1.0)
    )
    return (loss_scale * jnp.sum(live_mask * per_token), advantage)


def butterfly_sum(value, axis, size):
    step = 1
    while step < size:
        value = value + lax.ppermute(value, axis, [(i, i ^ step) for i in range(size)])
        step *= 2
    return value


def per_device(states, lengths, old_log_prob, up_weight, down_weight, score_head):
    shard_rows, seq_len, feature_width = states.shape
    up_block = up_weight[0]
    down_block = down_weight[0]
    head_block = score_head[0]
    head_fold = lax.psum(
        jnp.sum(down_block.astype(jnp.float32) * head_block[None, :], axis=1), "tp"
    )
    gathered = lax.all_gather(
        lax.all_gather(states, "dp", axis=0, tiled=True), "role", axis=0, tiled=True
    )
    tokens = gathered.reshape(-1, feature_width)
    partial_value = jnp.dot(tokens, up_block, preferred_element_type=jnp.float32)
    preact = lax.psum(partial_value.astype(jnp.bfloat16), "tp").astype(jnp.float32)
    activation = jax.nn.silu(preact).astype(jnp.bfloat16)
    branch = jnp.sum(activation.astype(jnp.float32) * head_fold[None, :], axis=1)
    leading = (lax.axis_index("dp") == 0).astype(jnp.float32)
    first_tp = (lax.axis_index("tp") == 0).astype(jnp.float32)
    direct = jnp.sum(tokens.astype(jnp.float32) * head_block[None, :], axis=1)
    own_terms = first_tp * branch + leading * direct
    role_count = lax.axis_size("role")
    picker = (jnp.arange(role_count, dtype=jnp.int32) == lax.axis_index("role")).astype(jnp.float32)
    scores = picker[:, None] * own_terms[None, :]
    for axis in ("tp", "dp", "role"):
        scores = butterfly_sum(scores, axis, lax.axis_size(axis))
    slopes, advantage = jax.grad(objective, has_aux=True)(scores, lengths, old_log_prob)
    cotangent = jnp.sum(slopes * picker[:, None], axis=0)
    upstream = (cotangent[:, None] * head_block[None, :]).astype(jnp.bfloat16)
    backflow = cotangent[:, None] * head_fold[None, :]
    sigmoid_value = jax.nn.sigmoid(preact)
    grad_pre = (backflow * sigmoid_value * (1.0 + preact * (1.0 - sigmoid_value))).astype(
        jnp.bfloat16
    )
    local = lax.dot_general(
        grad_pre, up_block, (((1,), (1,)), ((), ())), preferred_element_type=jnp.float32
    )
    row_groups = lax.axis_size(("role", "dp"))
    contrib = (local + leading * upstream.astype(jnp.float32)).astype(jnp.bfloat16)
    received = lax.all_to_all(
        contrib.reshape(row_groups, -1), ("role", "dp"), 0, 0, tiled=True
    )
    summed = jnp.sum(received.astype(jnp.float32), axis=0)
    return (advantage, summed.astype(jnp.bfloat16).reshape(shard_rows, seq_len, feature_width))


def solution(mesh):
    placed = (
        P(("role", "dp"), None, "tp"),
        P(),
        P(),
        P("role", "tp", "dp"),
        P("role", "dp", "tp"),
        P("role", "tp"),
    )
    return jax.shard_map(
        per_device,
        mesh=mesh,
        in_specs=placed,
        out_specs=(P(), P(("role", "dp"), None, "tp")),
        check_vma=False,
    )
```

```python
import jax
import jax.numpy as jnp
from jax import lax
from jax.sharding import PartitionSpec as P

penalty_beta = 0.05
trace_lambda = 0.95
value_weight = 0.5
kl_weight = 0.1
loss_scale = 64.0


def decay_table(seq_len):
    positions = jnp.arange(seq_len, dtype=jnp.int32)
    steps_ahead = positions[None, :] - positions[:, None]
    weights = jnp.power(jnp.float32(trace_lambda), jnp.maximum(steps_ahead, 0).astype(jnp.float32))
    return jnp.where(steps_ahead >= 0, weights, jnp.float32(0.0))


def objective(scores, lengths, old_log_prob):
    row_count, seq_len = old_log_prob.shape
    positions = jnp.arange(seq_len, dtype=jnp.int32)
    live_mask = (positions[None, :] < lengths[:, None]).astype(jnp.float32)
    final_pos = (positions[None, :] == lengths[:, None] - 1).astype(jnp.float32)
    score_grid = scores.reshape(scores.shape[0], row_count, seq_len)
    log_prob = jax.nn.log_sigmoid(score_grid[0])
    ref_log_prob = jax.nn.log_sigmoid(score_grid[1])
    value_est = score_grid[3]
    outcome = jnp.sum(score_grid[2] * final_pos, axis=1, keepdims=True)
    token_gain = live_mask * -penalty_beta * (log_prob - ref_log_prob) + final_pos * outcome
    frozen = live_mask * value_est
    next_value = jnp.concatenate([frozen[:, 1:], jnp.zeros((row_count, 1), jnp.float32)], axis=1)
    step_error = lax.stop_gradient(token_gain + next_value - frozen)
    advantage = live_mask * jnp.dot(
        step_error, decay_table(seq_len).T, precision=lax.Precision.HIGHEST
    )
    prob_ratio = jnp.exp(log_prob - old_log_prob)
    target = advantage + lax.stop_gradient(value_est)
    spread = ref_log_prob - log_prob
    per_token = (
        -prob_ratio * advantage
        + value_weight * 0.5 * (value_est - target) ** 2
        + kl_weight * (jnp.exp(spread) - spread - 1.0)
    )
    return (loss_scale * jnp.sum(live_mask * per_token), advantage)


def butterfly_sum(value, axis, size):
    step = 1
    while step < size:
        value = value + lax.ppermute(value, axis, [(i, i ^ step) for i in range(size)])
        step *= 2
    return value


def per_device(states, lengths, old_log_prob, up_weight, down_weight, score_head):
    shard_rows, seq_len, feature_width = states.shape
    up_block = up_weight[0]
    down_block = down_weight[0]
    head_block = score_head[0]
    hidden_width = up_block.shape[1]
    role_count = lax.axis_size("role")
    tp_count = lax.axis_size("tp")
    stage = lax.all_gather(states, "dp", axis=0, tiled=True)
    gathered = lax.all_to_all(
        jnp.broadcast_to(stage[None], (role_count,) + stage.shape), "role", 0, 0, tiled=True
    )
    tokens = gathered.reshape(-1, feature_width)
    token_count = tokens.shape[0]
    partial_value = jnp.dot(tokens, up_block, preferred_element_type=jnp.float32)
    fold_part = jnp.sum(down_block.astype(jnp.float32) * head_block[None, :], axis=1)
    direct_part = jnp.sum(tokens.astype(jnp.float32) * head_block[None, :], axis=1)
    extra_rows = 16
    extras = jnp.zeros((extra_rows, hidden_width), jnp.float32)
    extras = extras.at[0].set(fold_part).at[1, :token_count].set(direct_part)
    combined = jnp.concatenate([partial_value, extras], axis=0).astype(jnp.bfloat16)
    chunks = lax.all_to_all(
        combined.reshape(tp_count, -1, hidden_width), "tp", 0, 0, tiled=True
    )
    mine = jnp.sum(chunks.astype(jnp.float32), axis=0).astype(jnp.bfloat16)
    spread = lax.all_to_all(
        jnp.broadcast_to(mine[None], (tp_count,) + mine.shape), "tp", 0, 0, tiled=True
    )
    reduced = spread.reshape(-1, hidden_width).astype(jnp.float32)
    preact = reduced[:token_count]
    head_fold = reduced[token_count]
    direct = reduced[token_count + 1, :token_count]
    activation = jax.nn.silu(preact).astype(jnp.bfloat16)
    branch = jnp.sum(activation.astype(jnp.float32) * head_fold[None, :], axis=1)
    leading = (lax.axis_index("dp") == 0).astype(jnp.float32)
    own_terms = branch + leading * direct
    picker = (jnp.arange(role_count, dtype=jnp.int32) == lax.axis_index("role")).astype(jnp.float32)
    scores = picker[:, None] * own_terms[None, :]
    for axis in ("dp", "role"):
        scores = butterfly_sum(scores, axis, lax.axis_size(axis))
    slopes, advantage = jax.grad(objective, has_aux=True)(scores, lengths, old_log_prob)
    cotangent = jnp.sum(slopes * picker[:, None], axis=0)
    upstream = (cotangent[:, None] * head_block[None, :]).astype(jnp.bfloat16)
    backflow = cotangent[:, None] * head_fold[None, :]
    sigmoid_value = jax.nn.sigmoid(preact)
    grad_pre = (backflow * sigmoid_value * (1.0 + preact * (1.0 - sigmoid_value))).astype(
        jnp.bfloat16
    )
    local = lax.dot_general(
        grad_pre, up_block, (((1,), (1,)), ((), ())), preferred_element_type=jnp.float32
    )
    row_groups = lax.axis_size(("role", "dp"))
    contrib = (local + leading * upstream.astype(jnp.float32)).astype(jnp.bfloat16)
    received = lax.all_to_all(
        contrib.reshape(role_count, row_groups // role_count, -1), "role", 0, 0, tiled=True
    )
    received = jnp.sum(received.astype(jnp.float32), axis=0).astype(jnp.bfloat16)
    received = lax.all_to_all(received, "dp", 0, 0, tiled=True)
    summed = jnp.sum(received.astype(jnp.float32), axis=0)
    return (advantage, summed.astype(jnp.bfloat16).reshape(shard_rows, seq_len, feature_width))


def solution(mesh):
    placed = (
        P(("role", "dp"), None, "tp"),
        P(),
        P(),
        P("role", "tp", "dp"),
        P("role", "dp", "tp"),
        P("role", "tp"),
    )
    return jax.shard_map(
        per_device,
        mesh=mesh,
        in_specs=placed,
        out_specs=(P(), P(("role", "dp"), None, "tp")),
        check_vma=False,
    )
```

```python
import jax
import jax.numpy as jnp
from jax import lax
from jax.sharding import PartitionSpec as P

penalty_beta = 0.05
trace_lambda = 0.95
value_weight = 0.5
kl_weight = 0.1
loss_scale = 64.0


def decay_table(seq_len):
    positions = jnp.arange(seq_len, dtype=jnp.int32)
    steps_ahead = positions[None, :] - positions[:, None]
    weights = jnp.power(jnp.float32(trace_lambda), jnp.maximum(steps_ahead, 0).astype(jnp.float32))
    return jnp.where(steps_ahead >= 0, weights, jnp.float32(0.0))


def objective(scores, lengths, old_log_prob):
    row_count, seq_len = old_log_prob.shape
    positions = jnp.arange(seq_len, dtype=jnp.int32)
    live_mask = (positions[None, :] < lengths[:, None]).astype(jnp.float32)
    final_pos = (positions[None, :] == lengths[:, None] - 1).astype(jnp.float32)
    score_grid = scores.reshape(scores.shape[0], row_count, seq_len)
    log_prob = jax.nn.log_sigmoid(score_grid[0])
    ref_log_prob = jax.nn.log_sigmoid(score_grid[1])
    value_est = score_grid[3]
    outcome = jnp.sum(score_grid[2] * final_pos, axis=1, keepdims=True)
    token_gain = live_mask * -penalty_beta * (log_prob - ref_log_prob) + final_pos * outcome
    frozen = live_mask * value_est
    next_value = jnp.concatenate([frozen[:, 1:], jnp.zeros((row_count, 1), jnp.float32)], axis=1)
    step_error = lax.stop_gradient(token_gain + next_value - frozen)
    advantage = live_mask * jnp.dot(
        step_error, decay_table(seq_len).T, precision=lax.Precision.HIGHEST
    )
    prob_ratio = jnp.exp(log_prob - old_log_prob)
    target = advantage + lax.stop_gradient(value_est)
    spread = ref_log_prob - log_prob
    per_token = (
        -prob_ratio * advantage
        + value_weight * 0.5 * (value_est - target) ** 2
        + kl_weight * (jnp.exp(spread) - spread - 1.0)
    )
    return (loss_scale * jnp.sum(live_mask * per_token), advantage)


def per_device(states, lengths, old_log_prob, up_weight, down_weight, score_head):
    shard_rows, seq_len, feature_width = states.shape
    up_block = up_weight[0]
    down_block = down_weight[0]
    head_block = score_head[0]
    hidden_width = up_block.shape[1]
    role_count = lax.axis_size("role")
    tp_count = lax.axis_size("tp")
    stage = lax.all_gather(states, "dp", axis=0, tiled=True)
    gathered = lax.all_to_all(
        jnp.broadcast_to(stage[None], (role_count,) + stage.shape), "role", 0, 0, tiled=True
    )
    tokens = gathered.reshape(-1, feature_width)
    token_count = tokens.shape[0]
    partial_value = jnp.dot(tokens, up_block, preferred_element_type=jnp.float32)
    fold_part = jnp.sum(down_block.astype(jnp.float32) * head_block[None, :], axis=1)
    direct_part = jnp.sum(tokens.astype(jnp.float32) * head_block[None, :], axis=1)
    extra_rows = 16
    extras = jnp.zeros((extra_rows, hidden_width), jnp.float32)
    extras = extras.at[0].set(fold_part).at[1, :token_count].set(direct_part)
    combined = jnp.concatenate([partial_value, extras], axis=0).astype(jnp.bfloat16)
    chunks = lax.all_to_all(
        combined.reshape(tp_count, -1, hidden_width), "tp", 0, 0, tiled=True
    )
    mine = jnp.sum(chunks.astype(jnp.float32), axis=0).astype(jnp.bfloat16)
    spread = lax.all_to_all(
        jnp.broadcast_to(mine[None], (tp_count,) + mine.shape), "tp", 0, 0, tiled=True
    )
    reduced = spread.reshape(-1, hidden_width).astype(jnp.float32)
    preact = reduced[:token_count]
    head_fold = reduced[token_count]
    direct = reduced[token_count + 1, :token_count]
    activation = jax.nn.silu(preact).astype(jnp.bfloat16)
    branch = jnp.sum(activation.astype(jnp.float32) * head_fold[None, :], axis=1)
    leading = (lax.axis_index("dp") == 0).astype(jnp.float32)
    own_terms = branch + leading * direct
    picker = (jnp.arange(role_count, dtype=jnp.int32) == lax.axis_index("role")).astype(jnp.float32)
    row_groups = lax.axis_size(("role", "dp"))
    pieces = lax.all_to_all(
        jnp.broadcast_to(own_terms[None, :], (row_groups, token_count)),
        ("role", "dp"), 0, 0, tiled=True,
    )
    scores = jnp.sum(pieces.reshape(role_count, row_groups // role_count, token_count), axis=1)
    slopes, advantage = jax.grad(objective, has_aux=True)(scores, lengths, old_log_prob)
    cotangent = jnp.sum(slopes * picker[:, None], axis=0)
    upstream = (cotangent[:, None] * head_block[None, :]).astype(jnp.bfloat16)
    backflow = cotangent[:, None] * head_fold[None, :]
    sigmoid_value = jax.nn.sigmoid(preact)
    grad_pre = (backflow * sigmoid_value * (1.0 + preact * (1.0 - sigmoid_value))).astype(
        jnp.bfloat16
    )
    local = lax.dot_general(
        grad_pre, up_block, (((1,), (1,)), ((), ())), preferred_element_type=jnp.float32
    )
    contrib = (local + leading * upstream.astype(jnp.float32)).astype(jnp.bfloat16)
    received = lax.all_to_all(
        contrib.reshape(role_count, row_groups // role_count, -1), "role", 0, 0, tiled=True
    )
    received = jnp.sum(received.astype(jnp.float32), axis=0).astype(jnp.bfloat16)
    received = lax.all_to_all(received, "dp", 0, 0, tiled=True)
    summed = jnp.sum(received.astype(jnp.float32), axis=0)
    return (advantage, summed.astype(jnp.bfloat16).reshape(shard_rows, seq_len, feature_width))


def solution(mesh):
    placed = (
        P(("role", "dp"), None, "tp"),
        P(),
        P(),
        P("role", "tp", "dp"),
        P("role", "dp", "tp"),
        P("role", "tp"),
    )
    return jax.shard_map(
        per_device,
        mesh=mesh,
        in_specs=placed,
        out_specs=(P(), P(("role", "dp"), None, "tp")),
        check_vma=False,
    )
```

```python
import jax
import jax.numpy as jnp
from jax import lax
from jax.sharding import PartitionSpec as P

penalty_beta = 0.05
trace_lambda = 0.95
value_weight = 0.5
kl_weight = 0.1
loss_scale = 64.0


def decay_table(seq_len):
    positions = jnp.arange(seq_len, dtype=jnp.int32)
    steps_ahead = positions[None, :] - positions[:, None]
    weights = jnp.power(jnp.float32(trace_lambda), jnp.maximum(steps_ahead, 0).astype(jnp.float32))
    return jnp.where(steps_ahead >= 0, weights, jnp.float32(0.0))


def objective(scores, lengths, old_log_prob):
    row_count, seq_len = old_log_prob.shape
    positions = jnp.arange(seq_len, dtype=jnp.int32)
    live_mask = (positions[None, :] < lengths[:, None]).astype(jnp.float32)
    final_pos = (positions[None, :] == lengths[:, None] - 1).astype(jnp.float32)
    score_grid = scores.reshape(scores.shape[0], row_count, seq_len)
    log_prob = jax.nn.log_sigmoid(score_grid[0])
    ref_log_prob = jax.nn.log_sigmoid(score_grid[1])
    value_est = score_grid[3]
    outcome = jnp.sum(score_grid[2] * final_pos, axis=1, keepdims=True)
    token_gain = live_mask * -penalty_beta * (log_prob - ref_log_prob) + final_pos * outcome
    frozen = live_mask * value_est
    next_value = jnp.concatenate([frozen[:, 1:], jnp.zeros((row_count, 1), jnp.float32)], axis=1)
    step_error = lax.stop_gradient(token_gain + next_value - frozen)
    advantage = live_mask * jnp.dot(
        step_error, decay_table(seq_len).T, precision=lax.Precision.HIGHEST
    )
    prob_ratio = jnp.exp(log_prob - old_log_prob)
    target = advantage + lax.stop_gradient(value_est)
    spread = ref_log_prob - log_prob
    per_token = (
        -prob_ratio * advantage
        + value_weight * 0.5 * (value_est - target) ** 2
        + kl_weight * (jnp.exp(spread) - spread - 1.0)
    )
    return (loss_scale * jnp.sum(live_mask * per_token), advantage)


def per_device(states, lengths, old_log_prob, up_weight, down_weight, score_head):
    shard_rows, seq_len, feature_width = states.shape
    up_block = up_weight[0]
    down_block = down_weight[0]
    head_block = score_head[0]
    hidden_width = up_block.shape[1]
    role_count = lax.axis_size("role")
    tp_count = lax.axis_size("tp")
    stage = lax.all_gather(states.reshape(-1, feature_width), "dp", axis=0, tiled=True)
    gathered = lax.all_to_all(
        jnp.broadcast_to(stage[None], (role_count,) + stage.shape), "role", 0, 0, tiled=True
    )
    tokens = gathered.reshape(-1, feature_width)
    token_count = tokens.shape[0]
    partial_value = jnp.dot(tokens, up_block, preferred_element_type=jnp.float32)
    fold_part = jnp.sum(down_block.astype(jnp.float32) * head_block[None, :], axis=1)
    direct_part = jnp.sum(tokens.astype(jnp.float32) * head_block[None, :], axis=1)
    extra_rows = 16
    extras = jnp.zeros((extra_rows, hidden_width), jnp.float32)
    extras = extras.at[0].set(fold_part).at[1, :token_count].set(direct_part)
    combined = jnp.concatenate([partial_value, extras], axis=0).astype(jnp.bfloat16)
    chunks = lax.all_to_all(
        combined.reshape(tp_count, -1, hidden_width), "tp", 0, 0, tiled=True
    )
    mine = jnp.sum(chunks.astype(jnp.float32), axis=0).astype(jnp.bfloat16)
    spread = lax.all_to_all(
        jnp.broadcast_to(mine[None], (tp_count,) + mine.shape), "tp", 0, 0, tiled=True
    )
    reduced = spread.reshape(-1, hidden_width).astype(jnp.float32)
    preact = reduced[:token_count]
    head_fold = reduced[token_count]
    direct = reduced[token_count + 1, :token_count]
    activation = jax.nn.silu(preact).astype(jnp.bfloat16)
    branch = jnp.sum(activation.astype(jnp.float32) * head_fold[None, :], axis=1)
    leading = (lax.axis_index("dp") == 0).astype(jnp.float32)
    own_terms = branch + leading * direct
    picker = (jnp.arange(role_count, dtype=jnp.int32) == lax.axis_index("role")).astype(jnp.float32)
    row_groups = lax.axis_size(("role", "dp"))
    pieces = lax.all_to_all(
        jnp.broadcast_to(own_terms[None, :], (row_groups, token_count)),
        ("role", "dp"), 0, 0, tiled=True,
    )
    scores = jnp.sum(pieces.reshape(role_count, row_groups // role_count, token_count), axis=1)
    slopes, advantage = jax.grad(objective, has_aux=True)(scores, lengths, old_log_prob)
    cotangent = jnp.sum(slopes * picker[:, None], axis=0)
    upstream = (cotangent[:, None] * head_block[None, :]).astype(jnp.bfloat16)
    backflow = cotangent[:, None] * head_fold[None, :]
    sigmoid_value = jax.nn.sigmoid(preact)
    grad_pre = (backflow * sigmoid_value * (1.0 + preact * (1.0 - sigmoid_value))).astype(
        jnp.bfloat16
    )
    local = lax.dot_general(
        grad_pre, up_block, (((1,), (1,)), ((), ())), preferred_element_type=jnp.float32
    )
    contrib = (local + leading * upstream.astype(jnp.float32)).astype(jnp.bfloat16)
    received = lax.all_to_all(
        contrib.reshape(role_count, -1, feature_width), "role", 0, 0, tiled=True
    )
    received = jnp.sum(received.astype(jnp.float32), axis=0).astype(jnp.bfloat16)
    received = lax.all_to_all(
        received.reshape(row_groups // role_count, -1), "dp", 0, 0, tiled=True
    )
    summed = jnp.sum(received.astype(jnp.float32), axis=0)
    return (advantage, summed.astype(jnp.bfloat16).reshape(shard_rows, seq_len, feature_width))


def solution(mesh):
    placed = (
        P(("role", "dp"), None, "tp"),
        P(),
        P(),
        P("role", "tp", "dp"),
        P("role", "dp", "tp"),
        P("role", "tp"),
    )
    return jax.shard_map(
        per_device,
        mesh=mesh,
        in_specs=placed,
        out_specs=(P(), P(("role", "dp"), None, "tp")),
        check_vma=False,
    )
```

```python
import jax
import jax.numpy as jnp
from jax import lax
from jax.sharding import PartitionSpec as P

penalty_beta = 0.05
trace_lambda = 0.95
value_weight = 0.5
kl_weight = 0.1
loss_scale = 64.0


def decay_table(seq_len):
    positions = jnp.arange(seq_len, dtype=jnp.int32)
    steps_ahead = positions[None, :] - positions[:, None]
    weights = jnp.power(jnp.float32(trace_lambda), jnp.maximum(steps_ahead, 0).astype(jnp.float32))
    return jnp.where(steps_ahead >= 0, weights, jnp.float32(0.0))


def objective(scores, lengths, old_log_prob):
    row_count, seq_len = old_log_prob.shape
    positions = jnp.arange(seq_len, dtype=jnp.int32)
    live_mask = (positions[None, :] < lengths[:, None]).astype(jnp.float32)
    final_pos = (positions[None, :] == lengths[:, None] - 1).astype(jnp.float32)
    score_grid = scores.reshape(scores.shape[0], row_count, seq_len)
    log_prob = jax.nn.log_sigmoid(score_grid[0])
    ref_log_prob = jax.nn.log_sigmoid(score_grid[1])
    value_est = score_grid[3]
    outcome = jnp.sum(score_grid[2] * final_pos, axis=1, keepdims=True)
    token_gain = live_mask * -penalty_beta * (log_prob - ref_log_prob) + final_pos * outcome
    frozen = live_mask * value_est
    next_value = jnp.concatenate([frozen[:, 1:], jnp.zeros((row_count, 1), jnp.float32)], axis=1)
    step_error = lax.stop_gradient(token_gain + next_value - frozen)
    advantage = live_mask * jnp.dot(
        step_error, decay_table(seq_len).T, precision=lax.Precision.HIGHEST
    )
    prob_ratio = jnp.exp(log_prob - old_log_prob)
    target = advantage + lax.stop_gradient(value_est)
    spread = ref_log_prob - log_prob
    per_token = (
        -prob_ratio * advantage
        + value_weight * 0.5 * (value_est - target) ** 2
        + kl_weight * (jnp.exp(spread) - spread - 1.0)
    )
    return (loss_scale * jnp.sum(live_mask * per_token), advantage)


def per_device(states, lengths, old_log_prob, up_weight, down_weight, score_head):
    shard_rows, seq_len, feature_width = states.shape
    up_block = up_weight[0]
    down_block = down_weight[0]
    head_block = score_head[0]
    hidden_width = up_block.shape[1]
    role_count = lax.axis_size("role")
    tp_count = lax.axis_size("tp")
    stage = lax.all_gather(states.reshape(-1, feature_width), "dp", axis=0, tiled=True)
    gathered = lax.all_to_all(
        jnp.broadcast_to(stage[None], (role_count,) + stage.shape), "role", 0, 0, tiled=True
    )
    tokens = gathered.reshape(-1, feature_width)
    token_count = tokens.shape[0]
    partial_value = jnp.dot(tokens, up_block, preferred_element_type=jnp.float32)
    fold_part = jnp.sum(down_block.astype(jnp.float32) * head_block[None, :], axis=1)
    direct_part = jnp.sum(tokens.astype(jnp.float32) * head_block[None, :], axis=1)
    chunk_tokens = token_count // tp_count
    fold_rows = jnp.broadcast_to(fold_part[None, None, :], (tp_count, 1, hidden_width))
    direct_rows = jnp.pad(
        direct_part.reshape(tp_count, 1, chunk_tokens),
        ((0, 0), (0, 0), (0, hidden_width - chunk_tokens)),
    )
    combined = jnp.concatenate(
        [
            partial_value.astype(jnp.bfloat16).reshape(tp_count, chunk_tokens, hidden_width),
            fold_rows.astype(jnp.bfloat16),
            direct_rows.astype(jnp.bfloat16),
        ],
        axis=1,
    )
    chunks = lax.all_to_all(combined, "tp", 0, 0, tiled=True)
    mine = jnp.sum(chunks.astype(jnp.float32), axis=0).astype(jnp.bfloat16)
    spread = lax.all_to_all(
        jnp.broadcast_to(mine[None], (tp_count,) + mine.shape), "tp", 0, 0, tiled=True
    )
    preact = spread[:, :chunk_tokens].reshape(token_count, hidden_width).astype(jnp.float32)
    head_fold = spread[0, chunk_tokens].astype(jnp.float32)
    direct = spread[:, chunk_tokens + 1, :chunk_tokens].reshape(token_count).astype(jnp.float32)
    activation = jax.nn.silu(preact).astype(jnp.bfloat16)
    branch = jnp.sum(activation.astype(jnp.float32) * head_fold[None, :], axis=1)
    leading = (lax.axis_index("dp") == 0).astype(jnp.float32)
    own_terms = branch + leading * direct
    picker = (jnp.arange(role_count, dtype=jnp.int32) == lax.axis_index("role")).astype(jnp.float32)
    row_groups = lax.axis_size(("role", "dp"))
    pieces = lax.all_to_all(
        jnp.broadcast_to(own_terms[None, :], (row_groups, token_count)),
        ("role", "dp"), 0, 0, tiled=True,
    )
    scores = jnp.sum(pieces.reshape(role_count, row_groups // role_count, token_count), axis=1)
    slopes, advantage = jax.grad(objective, has_aux=True)(scores, lengths, old_log_prob)
    cotangent = jnp.sum(slopes * picker[:, None], axis=0)
    upstream = (cotangent[:, None] * head_block[None, :]).astype(jnp.bfloat16)
    backflow = cotangent[:, None] * head_fold[None, :]
    sigmoid_value = jax.nn.sigmoid(preact)
    grad_pre = (backflow * sigmoid_value * (1.0 + preact * (1.0 - sigmoid_value))).astype(
        jnp.bfloat16
    )
    local = lax.dot_general(
        grad_pre, up_block, (((1,), (1,)), ((), ())), preferred_element_type=jnp.float32
    )
    contrib = (local + leading * upstream.astype(jnp.float32)).astype(jnp.bfloat16)
    received = lax.all_to_all(
        contrib.reshape(role_count, -1, feature_width), "role", 0, 0, tiled=True
    )
    received = jnp.sum(received.astype(jnp.float32), axis=0).astype(jnp.bfloat16)
    received = lax.all_to_all(
        received.reshape(row_groups // role_count, -1), "dp", 0, 0, tiled=True
    )
    summed = jnp.sum(received.astype(jnp.float32), axis=0)
    return (advantage, summed.astype(jnp.bfloat16).reshape(shard_rows, seq_len, feature_width))


def solution(mesh):
    placed = (
        P(("role", "dp"), None, "tp"),
        P(),
        P(),
        P("role", "tp", "dp"),
        P("role", "dp", "tp"),
        P("role", "tp"),
    )
    return jax.shard_map(
        per_device,
        mesh=mesh,
        in_specs=placed,
        out_specs=(P(), P(("role", "dp"), None, "tp")),
        check_vma=False,
    )
```

```python
import jax
import jax.numpy as jnp
from jax import lax
from jax.sharding import PartitionSpec as P

penalty_beta = 0.05
trace_lambda = 0.95
value_weight = 0.5
kl_weight = 0.1
loss_scale = 64.0


def decay_table(seq_len):
    positions = jnp.arange(seq_len, dtype=jnp.int32)
    steps_ahead = positions[None, :] - positions[:, None]
    weights = jnp.power(jnp.float32(trace_lambda), jnp.maximum(steps_ahead, 0).astype(jnp.float32))
    return jnp.where(steps_ahead >= 0, weights, jnp.float32(0.0))


def objective(scores, lengths, old_log_prob):
    row_count, seq_len = old_log_prob.shape
    positions = jnp.arange(seq_len, dtype=jnp.int32)
    live_mask = (positions[None, :] < lengths[:, None]).astype(jnp.float32)
    final_pos = (positions[None, :] == lengths[:, None] - 1).astype(jnp.float32)
    score_grid = scores.reshape(scores.shape[0], row_count, seq_len)
    log_prob = jax.nn.log_sigmoid(score_grid[0])
    ref_log_prob = jax.nn.log_sigmoid(score_grid[1])
    value_est = score_grid[3]
    outcome = jnp.sum(score_grid[2] * final_pos, axis=1, keepdims=True)
    token_gain = live_mask * -penalty_beta * (log_prob - ref_log_prob) + final_pos * outcome
    frozen = live_mask * value_est
    next_value = jnp.concatenate([frozen[:, 1:], jnp.zeros((row_count, 1), jnp.float32)], axis=1)
    step_error = lax.stop_gradient(token_gain + next_value - frozen)
    advantage = live_mask * jnp.dot(
        step_error, decay_table(seq_len).T, precision=lax.Precision.HIGHEST
    )
    prob_ratio = jnp.exp(log_prob - old_log_prob)
    target = advantage + lax.stop_gradient(value_est)
    spread = ref_log_prob - log_prob
    per_token = (
        -prob_ratio * advantage
        + value_weight * 0.5 * (value_est - target) ** 2
        + kl_weight * (jnp.exp(spread) - spread - 1.0)
    )
    return (loss_scale * jnp.sum(live_mask * per_token), advantage)


def per_device(states, lengths, old_log_prob, up_weight, down_weight, score_head):
    shard_rows, seq_len, feature_width = states.shape
    up_block = up_weight[0]
    down_block = down_weight[0]
    head_block = score_head[0]
    hidden_width = up_block.shape[1]
    role_count = lax.axis_size("role")
    tp_count = lax.axis_size("tp")
    stage = lax.all_gather(states.reshape(-1, feature_width), "dp", axis=0, tiled=True)
    gathered = lax.all_to_all(
        jnp.broadcast_to(stage[None], (role_count,) + stage.shape), "role", 0, 0, tiled=True
    )
    tokens = gathered.reshape(-1, feature_width)
    token_count = tokens.shape[0]
    partial_value = jnp.dot(tokens, up_block, preferred_element_type=jnp.float32)
    fold_part = jnp.sum(down_block.astype(jnp.float32) * head_block[None, :], axis=1)
    direct_part = jnp.sum(tokens.astype(jnp.float32) * head_block[None, :], axis=1)
    chunk_tokens = token_count // tp_count
    fold_rows = jnp.broadcast_to(fold_part[None, None, :], (tp_count, 1, hidden_width))
    direct_rows = jnp.pad(
        direct_part.reshape(tp_count, 1, chunk_tokens),
        ((0, 0), (0, 0), (0, hidden_width - chunk_tokens)),
    )
    combined = jnp.concatenate(
        [
            partial_value.astype(jnp.bfloat16).reshape(tp_count, chunk_tokens, hidden_width),
            fold_rows.astype(jnp.bfloat16),
            direct_rows.astype(jnp.bfloat16),
        ],
        axis=1,
    )
    chunks = lax.all_to_all(combined.reshape(tp_count, -1), "tp", 0, 0, tiled=True)
    mine = jnp.sum(chunks.astype(jnp.float32), axis=0).astype(jnp.bfloat16)
    spread = lax.all_to_all(
        jnp.broadcast_to(mine[None], (tp_count,) + mine.shape), "tp", 0, 0, tiled=True
    ).reshape(combined.shape)
    preact = spread[:, :chunk_tokens].reshape(token_count, hidden_width).astype(jnp.float32)
    head_fold = spread[0, chunk_tokens].astype(jnp.float32)
    direct = spread[:, chunk_tokens + 1, :chunk_tokens].reshape(token_count).astype(jnp.float32)
    activation = jax.nn.silu(preact).astype(jnp.bfloat16)
    branch = jnp.sum(activation.astype(jnp.float32) * head_fold[None, :], axis=1)
    leading = (lax.axis_index("dp") == 0).astype(jnp.float32)
    own_terms = branch + leading * direct
    picker = (jnp.arange(role_count, dtype=jnp.int32) == lax.axis_index("role")).astype(jnp.float32)
    row_groups = lax.axis_size(("role", "dp"))
    pieces = lax.all_to_all(
        jnp.broadcast_to(own_terms[None, :], (row_groups, token_count)),
        ("role", "dp"), 0, 0, tiled=True,
    )
    scores = jnp.sum(pieces.reshape(role_count, row_groups // role_count, token_count), axis=1)
    slopes, advantage = jax.grad(objective, has_aux=True)(scores, lengths, old_log_prob)
    cotangent = jnp.sum(slopes * picker[:, None], axis=0)
    upstream = (cotangent[:, None] * head_block[None, :]).astype(jnp.bfloat16)
    backflow = cotangent[:, None] * head_fold[None, :]
    sigmoid_value = jax.nn.sigmoid(preact)
    grad_pre = (backflow * sigmoid_value * (1.0 + preact * (1.0 - sigmoid_value))).astype(
        jnp.bfloat16
    )
    local = lax.dot_general(
        grad_pre, up_block, (((1,), (1,)), ((), ())), preferred_element_type=jnp.float32
    )
    contrib = (local + leading * upstream.astype(jnp.float32)).astype(jnp.bfloat16)
    received = lax.all_to_all(
        contrib.reshape(role_count, -1, feature_width), "role", 0, 0, tiled=True
    )
    received = jnp.sum(received.astype(jnp.float32), axis=0).astype(jnp.bfloat16)
    received = lax.all_to_all(
        received.reshape(row_groups // role_count, -1), "dp", 0, 0, tiled=True
    )
    summed = jnp.sum(received.astype(jnp.float32), axis=0)
    return (advantage, summed.astype(jnp.bfloat16).reshape(shard_rows, seq_len, feature_width))


def solution(mesh):
    placed = (
        P(("role", "dp"), None, "tp"),
        P(),
        P(),
        P("role", "tp", "dp"),
        P("role", "dp", "tp"),
        P("role", "tp"),
    )
    return jax.shard_map(
        per_device,
        mesh=mesh,
        in_specs=placed,
        out_specs=(P(), P(("role", "dp"), None, "tp")),
        check_vma=False,
    )
```

```python
import jax
import jax.numpy as jnp
from jax import lax
from jax.sharding import PartitionSpec as P

penalty_beta = 0.05
trace_lambda = 0.95
value_weight = 0.5
kl_weight = 0.1
loss_scale = 64.0


def decay_table(seq_len):
    positions = jnp.arange(seq_len, dtype=jnp.int32)
    steps_ahead = positions[None, :] - positions[:, None]
    weights = jnp.power(jnp.float32(trace_lambda), jnp.maximum(steps_ahead, 0).astype(jnp.float32))
    return jnp.where(steps_ahead >= 0, weights, jnp.float32(0.0))


def objective(scores, lengths, old_log_prob):
    row_count, seq_len = old_log_prob.shape
    positions = jnp.arange(seq_len, dtype=jnp.int32)
    live_mask = (positions[None, :] < lengths[:, None]).astype(jnp.float32)
    final_pos = (positions[None, :] == lengths[:, None] - 1).astype(jnp.float32)
    score_grid = scores.reshape(scores.shape[0], row_count, seq_len)
    log_prob = jax.nn.log_sigmoid(score_grid[0])
    ref_log_prob = jax.nn.log_sigmoid(score_grid[1])
    value_est = score_grid[3]
    outcome = jnp.sum(score_grid[2] * final_pos, axis=1, keepdims=True)
    token_gain = live_mask * -penalty_beta * (log_prob - ref_log_prob) + final_pos * outcome
    frozen = live_mask * value_est
    next_value = jnp.concatenate([frozen[:, 1:], jnp.zeros((row_count, 1), jnp.float32)], axis=1)
    step_error = lax.stop_gradient(token_gain + next_value - frozen)
    advantage = live_mask * jnp.dot(
        step_error, decay_table(seq_len).T, precision=lax.Precision.HIGHEST
    )
    prob_ratio = jnp.exp(log_prob - old_log_prob)
    target = advantage + lax.stop_gradient(value_est)
    spread = ref_log_prob - log_prob
    per_token = (
        -prob_ratio * advantage
        + value_weight * 0.5 * (value_est - target) ** 2
        + kl_weight * (jnp.exp(spread) - spread - 1.0)
    )
    return (loss_scale * jnp.sum(live_mask * per_token), advantage)


def per_device(states, lengths, old_log_prob, up_weight, down_weight, score_head):
    shard_rows, seq_len, feature_width = states.shape
    up_block = up_weight[0]
    down_block = down_weight[0]
    head_block = score_head[0]
    hidden_width = up_block.shape[1]
    role_count = lax.axis_size("role")
    tp_count = lax.axis_size("tp")
    stage = lax.all_gather(states.reshape(-1, feature_width), "dp", axis=0, tiled=True)
    gathered = lax.all_to_all(
        jnp.broadcast_to(stage[None], (role_count,) + stage.shape), "role", 0, 0, tiled=True
    )
    tokens = gathered.reshape(-1, feature_width)
    token_count = tokens.shape[0]
    partial_value = jnp.dot(tokens, up_block, preferred_element_type=jnp.float32)
    fold_part = jnp.sum(down_block.astype(jnp.float32) * head_block[None, :], axis=1)
    direct_part = jnp.sum(tokens.astype(jnp.float32) * head_block[None, :], axis=1)
    chunk_tokens = token_count // tp_count
    fold_rows = jnp.broadcast_to(fold_part[None, None, :], (tp_count, 1, hidden_width))
    direct_rows = jnp.pad(
        direct_part.reshape(tp_count, 1, chunk_tokens),
        ((0, 0), (0, 0), (0, hidden_width - chunk_tokens)),
    )
    combined = jnp.concatenate(
        [
            partial_value.astype(jnp.bfloat16).reshape(tp_count, chunk_tokens, hidden_width),
            fold_rows.astype(jnp.bfloat16),
            direct_rows.astype(jnp.bfloat16),
        ],
        axis=1,
    )
    chunks = lax.all_to_all(combined, "tp", 0, 0, tiled=True)
    mine = jnp.sum(chunks.astype(jnp.float32), axis=0)
    preact = mine[:chunk_tokens]
    head_fold = mine[chunk_tokens]
    direct = mine[chunk_tokens + 1, :chunk_tokens]
    activation = jax.nn.silu(preact).astype(jnp.bfloat16)
    branch = jnp.sum(activation.astype(jnp.float32) * head_fold[None, :], axis=1)
    leading = (lax.axis_index("dp") == 0).astype(jnp.float32)
    own_terms = branch + leading * direct
    picker = (jnp.arange(role_count, dtype=jnp.int32) == lax.axis_index("role")).astype(jnp.float32)
    row_groups = lax.axis_size(("role", "dp"))
    pieces = lax.all_to_all(
        jnp.broadcast_to(own_terms[None, :], (row_groups, chunk_tokens)),
        ("role", "dp"), 0, 0, tiled=True,
    )
    scores = jnp.sum(pieces.reshape(role_count, row_groups // role_count, chunk_tokens), axis=1)
    chunk_rows = chunk_tokens // seq_len
    first_row = lax.axis_index("tp") * chunk_rows
    own_lengths = lax.dynamic_slice_in_dim(lengths, first_row, chunk_rows)
    own_old = lax.dynamic_slice_in_dim(old_log_prob, first_row, chunk_rows)
    slopes, own_advantage = jax.grad(objective, has_aux=True)(scores, own_lengths, own_old)
    own_slope = jnp.sum(slopes * picker[:, None], axis=0)
    sigmoid_value = jax.nn.sigmoid(preact)
    own_grad_pre = (
        own_slope[:, None] * head_fold[None, :] * sigmoid_value * (1.0 + preact * (1.0 - sigmoid_value))
    ).astype(jnp.bfloat16)
    side = jnp.stack([own_slope, own_advantage.reshape(chunk_tokens)])
    side_high = side.astype(jnp.bfloat16)
    side_low = (side - side_high.astype(jnp.float32)).astype(jnp.bfloat16)
    side_rows = jnp.pad(
        jnp.concatenate([side_high, side_low]), ((0, 0), (0, hidden_width - chunk_tokens))
    )
    payload = jnp.concatenate([own_grad_pre, side_rows], axis=0)
    spread = lax.all_to_all(
        jnp.broadcast_to(payload[None], (tp_count,) + payload.shape), "tp", 0, 0, tiled=True
    )
    grad_pre = spread[:, :chunk_tokens].reshape(token_count, hidden_width)
    side_all = (
        spread[:, chunk_tokens : chunk_tokens + 2, :chunk_tokens].astype(jnp.float32)
        + spread[:, chunk_tokens + 2 : chunk_tokens + 4, :chunk_tokens].astype(jnp.float32)
    )
    cotangent = side_all[:, 0].reshape(token_count)
    advantage = side_all[:, 1].reshape(lengths.shape[0], seq_len)
    upstream = (cotangent[:, None] * head_block[None, :]).astype(jnp.bfloat16)
    local = lax.dot_general(
        grad_pre, up_block, (((1,), (1,)), ((), ())), preferred_element_type=jnp.float32
    )
    contrib = (local + leading * upstream.astype(jnp.float32)).astype(jnp.bfloat16)
    received = lax.all_to_all(
        contrib.reshape(role_count, -1, feature_width), "role", 0, 0, tiled=True
    )
    received = jnp.sum(received.astype(jnp.float32), axis=0).astype(jnp.bfloat16)
    received = lax.all_to_all(
        received.reshape(row_groups // role_count, -1), "dp", 0, 0, tiled=True
    )
    summed = jnp.sum(received.astype(jnp.float32), axis=0)
    return (advantage, summed.astype(jnp.bfloat16).reshape(shard_rows, seq_len, feature_width))


def solution(mesh):
    placed = (
        P(("role", "dp"), None, "tp"),
        P(),
        P(),
        P("role", "tp", "dp"),
        P("role", "dp", "tp"),
        P("role", "tp"),
    )
    return jax.shard_map(
        per_device,
        mesh=mesh,
        in_specs=placed,
        out_specs=(P(), P(("role", "dp"), None, "tp")),
        check_vma=False,
    )
```

```python
import jax
import jax.numpy as jnp
from jax import lax
from jax.sharding import PartitionSpec as P

penalty_beta = 0.05
trace_lambda = 0.95
value_weight = 0.5
kl_weight = 0.1
loss_scale = 64.0


def decay_table(seq_len):
    positions = jnp.arange(seq_len, dtype=jnp.int32)
    steps_ahead = positions[None, :] - positions[:, None]
    weights = jnp.power(jnp.float32(trace_lambda), jnp.maximum(steps_ahead, 0).astype(jnp.float32))
    return jnp.where(steps_ahead >= 0, weights, jnp.float32(0.0))


def objective(scores, lengths, old_log_prob):
    row_count, seq_len = old_log_prob.shape
    positions = jnp.arange(seq_len, dtype=jnp.int32)
    live_mask = (positions[None, :] < lengths[:, None]).astype(jnp.float32)
    final_pos = (positions[None, :] == lengths[:, None] - 1).astype(jnp.float32)
    score_grid = scores.reshape(scores.shape[0], row_count, seq_len)
    log_prob = jax.nn.log_sigmoid(score_grid[0])
    ref_log_prob = jax.nn.log_sigmoid(score_grid[1])
    value_est = score_grid[3]
    outcome = jnp.sum(score_grid[2] * final_pos, axis=1, keepdims=True)
    token_gain = live_mask * -penalty_beta * (log_prob - ref_log_prob) + final_pos * outcome
    frozen = live_mask * value_est
    next_value = jnp.concatenate([frozen[:, 1:], jnp.zeros((row_count, 1), jnp.float32)], axis=1)
    step_error = lax.stop_gradient(token_gain + next_value - frozen)
    advantage = live_mask * jnp.dot(
        step_error, decay_table(seq_len).T, precision=lax.Precision.HIGHEST
    )
    prob_ratio = jnp.exp(log_prob - old_log_prob)
    target = advantage + lax.stop_gradient(value_est)
    spread = ref_log_prob - log_prob
    per_token = (
        -prob_ratio * advantage
        + value_weight * 0.5 * (value_est - target) ** 2
        + kl_weight * (jnp.exp(spread) - spread - 1.0)
    )
    return (loss_scale * jnp.sum(live_mask * per_token), advantage)


def per_device(states, lengths, old_log_prob, up_weight, down_weight, score_head):
    shard_rows, seq_len, feature_width = states.shape
    up_block = up_weight[0]
    down_block = down_weight[0]
    head_block = score_head[0]
    hidden_width = up_block.shape[1]
    role_count = lax.axis_size("role")
    tp_count = lax.axis_size("tp")
    stage = lax.all_gather(states.reshape(-1, feature_width), "dp", axis=0, tiled=True)
    gathered = lax.all_to_all(
        jnp.broadcast_to(stage[None], (role_count,) + stage.shape), "role", 0, 0, tiled=True
    )
    tokens = gathered.reshape(-1, feature_width)
    token_count = tokens.shape[0]
    partial_value = jnp.dot(tokens, up_block, preferred_element_type=jnp.float32)
    fold_part = jnp.sum(down_block.astype(jnp.float32) * head_block[None, :], axis=1)
    direct_part = jnp.sum(tokens.astype(jnp.float32) * head_block[None, :], axis=1)
    chunk_tokens = token_count // tp_count
    fold_rows = jnp.broadcast_to(fold_part[None, None, :], (tp_count, 1, hidden_width))
    direct_rows = jnp.pad(
        direct_part.reshape(tp_count, 1, chunk_tokens),
        ((0, 0), (0, 0), (0, hidden_width - chunk_tokens)),
    )
    side_rows = jnp.concatenate([fold_rows, direct_rows], axis=1)
    side_high = side_rows.astype(jnp.bfloat16)
    side_low = (side_rows - side_high.astype(jnp.float32)).astype(jnp.bfloat16)
    combined = jnp.concatenate(
        [
            partial_value.astype(jnp.bfloat16).reshape(tp_count, chunk_tokens, hidden_width),
            side_high,
            side_low,
        ],
        axis=1,
    )
    chunks = lax.all_to_all(combined, "tp", 0, 0, tiled=True)
    mine = jnp.sum(chunks.astype(jnp.float32), axis=0)
    preact = mine[:chunk_tokens]
    head_fold = mine[chunk_tokens] + mine[chunk_tokens + 2]
    direct = mine[chunk_tokens + 1, :chunk_tokens] + mine[chunk_tokens + 3, :chunk_tokens]
    activation = jax.nn.silu(preact).astype(jnp.bfloat16)
    branch = jnp.sum(activation.astype(jnp.float32) * head_fold[None, :], axis=1)
    leading = (lax.axis_index("dp") == 0).astype(jnp.float32)
    own_terms = branch + leading * direct
    picker = (jnp.arange(role_count, dtype=jnp.int32) == lax.axis_index("role")).astype(jnp.float32)
    row_groups = lax.axis_size(("role", "dp"))
    pieces = lax.all_to_all(
        jnp.broadcast_to(own_terms[None, :], (row_groups, chunk_tokens)),
        ("role", "dp"), 0, 0, tiled=True,
    )
    scores = jnp.sum(pieces.reshape(role_count, row_groups // role_count, chunk_tokens), axis=1)
    chunk_rows = chunk_tokens // seq_len
    first_row = lax.axis_index("tp") * chunk_rows
    own_lengths = lax.dynamic_slice_in_dim(lengths, first_row, chunk_rows)
    own_old = lax.dynamic_slice_in_dim(old_log_prob, first_row, chunk_rows)
    slopes, own_advantage = jax.grad(objective, has_aux=True)(scores, own_lengths, own_old)
    own_slope = jnp.sum(slopes * picker[:, None], axis=0)
    sigmoid_value = jax.nn.sigmoid(preact)
    own_grad_pre = (
        own_slope[:, None] * head_fold[None, :] * sigmoid_value * (1.0 + preact * (1.0 - sigmoid_value))
    ).astype(jnp.bfloat16)
    side = jnp.stack([own_slope, own_advantage.reshape(chunk_tokens)])
    side_high = side.astype(jnp.bfloat16)
    side_low = (side - side_high.astype(jnp.float32)).astype(jnp.bfloat16)
    side_rows = jnp.pad(
        jnp.concatenate([side_high, side_low]), ((0, 0), (0, hidden_width - chunk_tokens))
    )
    payload = jnp.concatenate([own_grad_pre, side_rows], axis=0)
    spread = lax.all_to_all(
        jnp.broadcast_to(payload[None], (tp_count,) + payload.shape), "tp", 0, 0, tiled=True
    )
    grad_pre = spread[:, :chunk_tokens].reshape(token_count, hidden_width)
    side_all = (
        spread[:, chunk_tokens : chunk_tokens + 2, :chunk_tokens].astype(jnp.float32)
        + spread[:, chunk_tokens + 2 : chunk_tokens + 4, :chunk_tokens].astype(jnp.float32)
    )
    cotangent = side_all[:, 0].reshape(token_count)
    advantage = side_all[:, 1].reshape(lengths.shape[0], seq_len)
    upstream = (cotangent[:, None] * head_block[None, :]).astype(jnp.bfloat16)
    local = lax.dot_general(
        grad_pre, up_block, (((1,), (1,)), ((), ())), preferred_element_type=jnp.float32
    )
    contrib = (local + leading * upstream.astype(jnp.float32)).astype(jnp.bfloat16)
    received = lax.all_to_all(
        contrib.reshape(role_count, -1, feature_width), "role", 0, 0, tiled=True
    )
    received = jnp.sum(received.astype(jnp.float32), axis=0).astype(jnp.bfloat16)
    received = lax.all_to_all(
        received.reshape(row_groups // role_count, -1), "dp", 0, 0, tiled=True
    )
    summed = jnp.sum(received.astype(jnp.float32), axis=0)
    return (advantage, summed.astype(jnp.bfloat16).reshape(shard_rows, seq_len, feature_width))


def solution(mesh):
    placed = (
        P(("role", "dp"), None, "tp"),
        P(),
        P(),
        P("role", "tp", "dp"),
        P("role", "dp", "tp"),
        P("role", "tp"),
    )
    return jax.shard_map(
        per_device,
        mesh=mesh,
        in_specs=placed,
        out_specs=(P(), P(("role", "dp"), None, "tp")),
        check_vma=False,
    )
```

```python
import jax
import jax.numpy as jnp
from jax import lax
from jax.sharding import PartitionSpec as P

penalty_beta = 0.05
trace_lambda = 0.95
value_weight = 0.5
kl_weight = 0.1
loss_scale = 64.0


def decay_table(seq_len):
    positions = jnp.arange(seq_len, dtype=jnp.int32)
    steps_ahead = positions[None, :] - positions[:, None]
    weights = jnp.power(jnp.float32(trace_lambda), jnp.maximum(steps_ahead, 0).astype(jnp.float32))
    return jnp.where(steps_ahead >= 0, weights, jnp.float32(0.0))


def objective(scores, lengths, old_log_prob):
    row_count, seq_len = old_log_prob.shape
    positions = jnp.arange(seq_len, dtype=jnp.int32)
    live_mask = (positions[None, :] < lengths[:, None]).astype(jnp.float32)
    final_pos = (positions[None, :] == lengths[:, None] - 1).astype(jnp.float32)
    score_grid = scores.reshape(scores.shape[0], row_count, seq_len)
    log_prob = jax.nn.log_sigmoid(score_grid[0])
    ref_log_prob = jax.nn.log_sigmoid(score_grid[1])
    value_est = score_grid[3]
    outcome = jnp.sum(score_grid[2] * final_pos, axis=1, keepdims=True)
    token_gain = live_mask * -penalty_beta * (log_prob - ref_log_prob) + final_pos * outcome
    frozen = live_mask * value_est
    next_value = jnp.concatenate([frozen[:, 1:], jnp.zeros((row_count, 1), jnp.float32)], axis=1)
    step_error = lax.stop_gradient(token_gain + next_value - frozen)
    advantage = live_mask * jnp.dot(
        step_error, decay_table(seq_len).T, precision=lax.Precision.HIGHEST
    )
    prob_ratio = jnp.exp(log_prob - old_log_prob)
    target = advantage + lax.stop_gradient(value_est)
    spread = ref_log_prob - log_prob
    per_token = (
        -prob_ratio * advantage
        + value_weight * 0.5 * (value_est - target) ** 2
        + kl_weight * (jnp.exp(spread) - spread - 1.0)
    )
    return (loss_scale * jnp.sum(live_mask * per_token), advantage)


def per_device(states, lengths, old_log_prob, up_weight, down_weight, score_head):
    shard_rows, seq_len, feature_width = states.shape
    up_block = up_weight[0]
    down_block = down_weight[0]
    head_block = score_head[0]
    hidden_width = up_block.shape[1]
    role_count = lax.axis_size("role")
    tp_count = lax.axis_size("tp")
    stage = lax.all_gather(states.reshape(-1, feature_width), "dp", axis=0, tiled=True)
    dp_count = lax.axis_size("dp")
    core = lax.axis_index("dp") % 2
    halves = stage.reshape(2, -1, feature_width)
    own_half = lax.dynamic_index_in_dim(halves, core, 0, keepdims=False)
    got = lax.all_to_all(
        jnp.broadcast_to(own_half[None], (role_count,) + own_half.shape), "role", 0, 0, tiled=True
    )
    other = lax.ppermute(got, "dp", [(i, i ^ 1) for i in range(dp_count)])
    gathered = jnp.where(
        core == 0, jnp.concatenate([got, other], axis=1), jnp.concatenate([other, got], axis=1)
    )
    tokens = gathered.reshape(-1, feature_width)
    token_count = tokens.shape[0]
    partial_value = jnp.dot(tokens, up_block, preferred_element_type=jnp.float32)
    fold_part = jnp.sum(down_block.astype(jnp.float32) * head_block[None, :], axis=1)
    direct_part = jnp.sum(tokens.astype(jnp.float32) * head_block[None, :], axis=1)
    chunk_tokens = token_count // tp_count
    fold_rows = jnp.broadcast_to(fold_part[None, None, :], (tp_count, 1, hidden_width))
    direct_rows = jnp.pad(
        direct_part.reshape(tp_count, 1, chunk_tokens),
        ((0, 0), (0, 0), (0, hidden_width - chunk_tokens)),
    )
    side_rows = jnp.concatenate([fold_rows, direct_rows], axis=1)
    side_high = side_rows.astype(jnp.bfloat16)
    side_low = (side_rows - side_high.astype(jnp.float32)).astype(jnp.bfloat16)
    combined = jnp.concatenate(
        [
            partial_value.astype(jnp.bfloat16).reshape(tp_count, chunk_tokens, hidden_width),
            side_high,
            side_low,
        ],
        axis=1,
    )
    chunks = lax.all_to_all(combined, "tp", 0, 0, tiled=True)
    mine = jnp.sum(chunks.astype(jnp.float32), axis=0)
    preact = mine[:chunk_tokens]
    head_fold = mine[chunk_tokens] + mine[chunk_tokens + 2]
    direct = mine[chunk_tokens + 1, :chunk_tokens] + mine[chunk_tokens + 3, :chunk_tokens]
    activation = jax.nn.silu(preact).astype(jnp.bfloat16)
    branch = jnp.sum(activation.astype(jnp.float32) * head_fold[None, :], axis=1)
    leading = (lax.axis_index("dp") == 0).astype(jnp.float32)
    own_terms = branch + leading * direct
    picker = (jnp.arange(role_count, dtype=jnp.int32) == lax.axis_index("role")).astype(jnp.float32)
    row_groups = lax.axis_size(("role", "dp"))
    pieces = lax.all_to_all(
        jnp.broadcast_to(own_terms[None, :], (row_groups, chunk_tokens)),
        ("role", "dp"), 0, 0, tiled=True,
    )
    scores = jnp.sum(pieces.reshape(role_count, row_groups // role_count, chunk_tokens), axis=1)
    chunk_rows = chunk_tokens // seq_len
    first_row = lax.axis_index("tp") * chunk_rows
    own_lengths = lax.dynamic_slice_in_dim(lengths, first_row, chunk_rows)
    own_old = lax.dynamic_slice_in_dim(old_log_prob, first_row, chunk_rows)
    slopes, own_advantage = jax.grad(objective, has_aux=True)(scores, own_lengths, own_old)
    own_slope = jnp.sum(slopes * picker[:, None], axis=0)
    sigmoid_value = jax.nn.sigmoid(preact)
    own_grad_pre = (
        own_slope[:, None] * head_fold[None, :] * sigmoid_value * (1.0 + preact * (1.0 - sigmoid_value))
    ).astype(jnp.bfloat16)
    side = jnp.stack([own_slope, own_advantage.reshape(chunk_tokens)])
    side_high = side.astype(jnp.bfloat16)
    side_low = (side - side_high.astype(jnp.float32)).astype(jnp.bfloat16)
    side_rows = jnp.pad(
        jnp.concatenate([side_high, side_low]), ((0, 0), (0, hidden_width - chunk_tokens))
    )
    payload = jnp.concatenate([own_grad_pre, side_rows], axis=0)
    spread = lax.all_to_all(
        jnp.broadcast_to(payload[None], (tp_count,) + payload.shape), "tp", 0, 0, tiled=True
    )
    grad_pre = spread[:, :chunk_tokens].reshape(token_count, hidden_width)
    side_all = (
        spread[:, chunk_tokens : chunk_tokens + 2, :chunk_tokens].astype(jnp.float32)
        + spread[:, chunk_tokens + 2 : chunk_tokens + 4, :chunk_tokens].astype(jnp.float32)
    )
    cotangent = side_all[:, 0].reshape(token_count)
    advantage = side_all[:, 1].reshape(lengths.shape[0], seq_len)
    upstream = (cotangent[:, None] * head_block[None, :]).astype(jnp.bfloat16)
    local = lax.dot_general(
        grad_pre, up_block, (((1,), (1,)), ((), ())), preferred_element_type=jnp.float32
    )
    contrib = (local + leading * upstream.astype(jnp.float32)).astype(jnp.bfloat16)
    received = lax.all_to_all(
        contrib.reshape(role_count, -1, feature_width), "role", 0, 0, tiled=True
    )
    received = jnp.sum(received.astype(jnp.float32), axis=0).astype(jnp.bfloat16)
    received = lax.all_to_all(
        received.reshape(row_groups // role_count, -1), "dp", 0, 0, tiled=True
    )
    summed = jnp.sum(received.astype(jnp.float32), axis=0)
    return (advantage, summed.astype(jnp.bfloat16).reshape(shard_rows, seq_len, feature_width))


def solution(mesh):
    placed = (
        P(("role", "dp"), None, "tp"),
        P(),
        P(),
        P("role", "tp", "dp"),
        P("role", "dp", "tp"),
        P("role", "tp"),
    )
    return jax.shard_map(
        per_device,
        mesh=mesh,
        in_specs=placed,
        out_specs=(P(), P(("role", "dp"), None, "tp")),
        check_vma=False,
    )
```

```python
import jax
import jax.numpy as jnp
from jax import lax
from jax.sharding import PartitionSpec as P

penalty_beta = 0.05
trace_lambda = 0.95
value_weight = 0.5
kl_weight = 0.1
loss_scale = 64.0


def decay_table(seq_len):
    positions = jnp.arange(seq_len, dtype=jnp.int32)
    steps_ahead = positions[None, :] - positions[:, None]
    weights = jnp.power(jnp.float32(trace_lambda), jnp.maximum(steps_ahead, 0).astype(jnp.float32))
    return jnp.where(steps_ahead >= 0, weights, jnp.float32(0.0))


def objective(scores, lengths, old_log_prob):
    row_count, seq_len = old_log_prob.shape
    positions = jnp.arange(seq_len, dtype=jnp.int32)
    live_mask = (positions[None, :] < lengths[:, None]).astype(jnp.float32)
    final_pos = (positions[None, :] == lengths[:, None] - 1).astype(jnp.float32)
    score_grid = scores.reshape(scores.shape[0], row_count, seq_len)
    log_prob = jax.nn.log_sigmoid(score_grid[0])
    ref_log_prob = jax.nn.log_sigmoid(score_grid[1])
    value_est = score_grid[3]
    outcome = jnp.sum(score_grid[2] * final_pos, axis=1, keepdims=True)
    token_gain = live_mask * -penalty_beta * (log_prob - ref_log_prob) + final_pos * outcome
    frozen = live_mask * value_est
    next_value = jnp.concatenate([frozen[:, 1:], jnp.zeros((row_count, 1), jnp.float32)], axis=1)
    step_error = lax.stop_gradient(token_gain + next_value - frozen)
    advantage = live_mask * jnp.dot(
        step_error, decay_table(seq_len).T, precision=lax.Precision.HIGHEST
    )
    prob_ratio = jnp.exp(log_prob - old_log_prob)
    target = advantage + lax.stop_gradient(value_est)
    spread = ref_log_prob - log_prob
    per_token = (
        -prob_ratio * advantage
        + value_weight * 0.5 * (value_est - target) ** 2
        + kl_weight * (jnp.exp(spread) - spread - 1.0)
    )
    return (loss_scale * jnp.sum(live_mask * per_token), advantage)


def per_device(states, lengths, old_log_prob, up_weight, down_weight, score_head):
    shard_rows, seq_len, feature_width = states.shape
    up_block = up_weight[0]
    down_block = down_weight[0]
    head_block = score_head[0]
    hidden_width = up_block.shape[1]
    role_count = lax.axis_size("role")
    tp_count = lax.axis_size("tp")
    stage = lax.all_gather(states.reshape(-1, feature_width), "dp", axis=0, tiled=True)
    dp_count = lax.axis_size("dp")
    core = lax.axis_index("dp") % 2
    halves = stage.reshape(2, -1, feature_width)
    own_half = lax.dynamic_index_in_dim(halves, core, 0, keepdims=False)
    got = lax.all_to_all(
        jnp.broadcast_to(own_half[None], (role_count,) + own_half.shape), "role", 0, 0, tiled=True
    )
    other = lax.ppermute(got, "dp", [(i, i ^ 1) for i in range(dp_count)])
    gathered = jnp.where(
        core == 0, jnp.concatenate([got, other], axis=1), jnp.concatenate([other, got], axis=1)
    )
    tokens = gathered.reshape(-1, feature_width)
    token_count = tokens.shape[0]
    partial_value = jnp.dot(tokens, up_block, preferred_element_type=jnp.float32)
    fold_part = jnp.sum(down_block.astype(jnp.float32) * head_block[None, :], axis=1)
    direct_part = jnp.sum(tokens.astype(jnp.float32) * head_block[None, :], axis=1)
    chunk_tokens = token_count // tp_count
    fold_rows = jnp.broadcast_to(fold_part[None, None, :], (tp_count, 1, hidden_width))
    direct_rows = jnp.pad(
        direct_part.reshape(tp_count, 1, chunk_tokens),
        ((0, 0), (0, 0), (0, hidden_width - chunk_tokens)),
    )
    side_rows = jnp.concatenate([fold_rows, direct_rows], axis=1)
    side_high = side_rows.astype(jnp.bfloat16)
    side_low = (side_rows - side_high.astype(jnp.float32)).astype(jnp.bfloat16)
    combined = jnp.concatenate(
        [
            partial_value.astype(jnp.bfloat16).reshape(tp_count, chunk_tokens, hidden_width),
            side_high,
            side_low,
        ],
        axis=1,
    )
    chunks = lax.all_to_all(combined, "tp", 0, 0, tiled=True)
    mine = jnp.sum(chunks.astype(jnp.float32), axis=0)
    preact = mine[:chunk_tokens]
    head_fold = mine[chunk_tokens] + mine[chunk_tokens + 2]
    direct = mine[chunk_tokens + 1, :chunk_tokens] + mine[chunk_tokens + 3, :chunk_tokens]
    activation = jax.nn.silu(preact).astype(jnp.bfloat16)
    branch = jnp.sum(activation.astype(jnp.float32) * head_fold[None, :], axis=1)
    leading = (lax.axis_index("dp") == 0).astype(jnp.float32)
    own_terms = branch + leading * direct
    picker = (jnp.arange(role_count, dtype=jnp.int32) == lax.axis_index("role")).astype(jnp.float32)
    row_groups = lax.axis_size(("role", "dp"))
    pieces = lax.all_to_all(
        jnp.broadcast_to(own_terms[None, :], (row_groups, chunk_tokens)),
        ("role", "dp"), 0, 0, tiled=True,
    )
    scores = jnp.sum(pieces.reshape(role_count, row_groups // role_count, chunk_tokens), axis=1)
    chunk_rows = chunk_tokens // seq_len
    first_row = lax.axis_index("tp") * chunk_rows
    own_lengths = lax.dynamic_slice_in_dim(lengths, first_row, chunk_rows)
    own_old = lax.dynamic_slice_in_dim(old_log_prob, first_row, chunk_rows)
    slopes, own_advantage = jax.grad(objective, has_aux=True)(scores, own_lengths, own_old)
    own_slope = jnp.sum(slopes * picker[:, None], axis=0)
    sigmoid_value = jax.nn.sigmoid(preact)
    own_grad_pre = (
        own_slope[:, None] * head_fold[None, :] * sigmoid_value * (1.0 + preact * (1.0 - sigmoid_value))
    ).astype(jnp.bfloat16)
    side = jnp.stack([own_slope, own_advantage.reshape(chunk_tokens)])
    side_high = side.astype(jnp.bfloat16)
    side_low = (side - side_high.astype(jnp.float32)).astype(jnp.bfloat16)
    side_rows = jnp.pad(
        jnp.concatenate([side_high, side_low]), ((0, 0), (0, hidden_width - chunk_tokens))
    )
    payload = jnp.concatenate([own_grad_pre, side_rows], axis=0)
    spread = lax.all_to_all(
        jnp.broadcast_to(payload[None], (tp_count,) + payload.shape), "tp", 0, 0, tiled=True
    )
    grad_pre = spread[:, :chunk_tokens].reshape(token_count, hidden_width)
    side_all = (
        spread[:, chunk_tokens : chunk_tokens + 2, :chunk_tokens].astype(jnp.float32)
        + spread[:, chunk_tokens + 2 : chunk_tokens + 4, :chunk_tokens].astype(jnp.float32)
    )
    cotangent = side_all[:, 0].reshape(token_count)
    advantage = side_all[:, 1].reshape(lengths.shape[0], seq_len)
    upstream = (cotangent[:, None] * head_block[None, :]).astype(jnp.bfloat16)
    local = lax.dot_general(
        grad_pre, up_block, (((1,), (1,)), ((), ())), preferred_element_type=jnp.float32
    )
    contrib = (local + leading * upstream.astype(jnp.float32)).astype(jnp.bfloat16)
    by_core = contrib.reshape(role_count, dp_count // 2, 2, -1)
    keep = lax.dynamic_index_in_dim(by_core, core, 2, keepdims=False)
    give = lax.dynamic_index_in_dim(by_core, 1 - core, 2, keepdims=False)
    taken = lax.ppermute(give, "dp", [(i, i ^ 1) for i in range(dp_count)])
    paired = (keep.astype(jnp.float32) + taken.astype(jnp.float32)).astype(jnp.bfloat16)
    received = lax.all_to_all(paired, "role", 0, 0, tiled=True)
    received = jnp.sum(received.astype(jnp.float32), axis=0).astype(jnp.bfloat16)
    blank = jnp.zeros_like(received)
    spaced = jnp.where(
        core == 0, jnp.stack([received, blank], axis=1), jnp.stack([blank, received], axis=1)
    )
    received = lax.all_to_all(spaced.reshape(dp_count, -1), "dp", 0, 0, tiled=True)
    summed = jnp.sum(received.astype(jnp.float32), axis=0)
    return (advantage, summed.astype(jnp.bfloat16).reshape(shard_rows, seq_len, feature_width))


def solution(mesh):
    placed = (
        P(("role", "dp"), None, "tp"),
        P(),
        P(),
        P("role", "tp", "dp"),
        P("role", "dp", "tp"),
        P("role", "tp"),
    )
    return jax.shard_map(
        per_device,
        mesh=mesh,
        in_specs=placed,
        out_specs=(P(), P(("role", "dp"), None, "tp")),
        check_vma=False,
    )
```

```python
import jax
import jax.numpy as jnp
from jax import lax
from jax.sharding import PartitionSpec as P

penalty_beta = 0.05
trace_lambda = 0.95
value_weight = 0.5
kl_weight = 0.1
loss_scale = 64.0


def decay_table(seq_len):
    positions = jnp.arange(seq_len, dtype=jnp.int32)
    steps_ahead = positions[None, :] - positions[:, None]
    weights = jnp.power(jnp.float32(trace_lambda), jnp.maximum(steps_ahead, 0).astype(jnp.float32))
    return jnp.where(steps_ahead >= 0, weights, jnp.float32(0.0))


def objective(scores, lengths, old_log_prob):
    row_count, seq_len = old_log_prob.shape
    positions = jnp.arange(seq_len, dtype=jnp.int32)
    live_mask = (positions[None, :] < lengths[:, None]).astype(jnp.float32)
    final_pos = (positions[None, :] == lengths[:, None] - 1).astype(jnp.float32)
    score_grid = scores.reshape(scores.shape[0], row_count, seq_len)
    log_prob = jax.nn.log_sigmoid(score_grid[0])
    ref_log_prob = jax.nn.log_sigmoid(score_grid[1])
    value_est = score_grid[3]
    outcome = jnp.sum(score_grid[2] * final_pos, axis=1, keepdims=True)
    token_gain = live_mask * -penalty_beta * (log_prob - ref_log_prob) + final_pos * outcome
    frozen = live_mask * value_est
    next_value = jnp.concatenate([frozen[:, 1:], jnp.zeros((row_count, 1), jnp.float32)], axis=1)
    step_error = lax.stop_gradient(token_gain + next_value - frozen)
    advantage = live_mask * jnp.dot(
        step_error, decay_table(seq_len).T, precision=lax.Precision.HIGHEST
    )
    prob_ratio = jnp.exp(log_prob - old_log_prob)
    target = advantage + lax.stop_gradient(value_est)
    spread = ref_log_prob - log_prob
    per_token = (
        -prob_ratio * advantage
        + value_weight * 0.5 * (value_est - target) ** 2
        + kl_weight * (jnp.exp(spread) - spread - 1.0)
    )
    return (loss_scale * jnp.sum(live_mask * per_token), advantage)


def per_device(states, lengths, old_log_prob, up_weight, down_weight, score_head):
    shard_rows, seq_len, feature_width = states.shape
    up_block = up_weight[0]
    down_block = down_weight[0]
    head_block = score_head[0]
    hidden_width = up_block.shape[1]
    role_count = lax.axis_size("role")
    tp_count = lax.axis_size("tp")
    stage = lax.all_gather(states.reshape(-1, feature_width), "dp", axis=0, tiled=True)
    dp_count = lax.axis_size("dp")
    core = lax.axis_index("dp") % 2
    halves = stage.reshape(2, -1, feature_width)
    own_half = lax.dynamic_index_in_dim(halves, core, 0, keepdims=False)
    got = lax.all_to_all(
        jnp.broadcast_to(own_half[None], (role_count,) + own_half.shape), "role", 0, 0, tiled=True
    )
    other = lax.ppermute(got, "dp", [(i, i ^ 1) for i in range(dp_count)])
    def project(half):
        flat = half.reshape(-1, feature_width)
        value = jnp.dot(flat, up_block, preferred_element_type=jnp.float32)
        direct_value = jnp.sum(flat.astype(jnp.float32) * head_block[None, :], axis=1)
        return value.reshape(role_count, -1, hidden_width), direct_value.reshape(role_count, -1)

    got_value, got_direct = project(got)
    other_value, other_direct = project(other)

    def in_order(mine_part, partner_part):
        return jnp.where(
            core == 0,
            jnp.concatenate([mine_part, partner_part], axis=1),
            jnp.concatenate([partner_part, mine_part], axis=1),
        )

    partial_value = in_order(got_value, other_value).reshape(-1, hidden_width)
    direct_part = in_order(got_direct, other_direct).reshape(-1)
    token_count = partial_value.shape[0]
    fold_part = jnp.sum(down_block.astype(jnp.float32) * head_block[None, :], axis=1)
    chunk_tokens = token_count // tp_count
    fold_rows = jnp.broadcast_to(fold_part[None, None, :], (tp_count, 1, hidden_width))
    direct_rows = jnp.pad(
        direct_part.reshape(tp_count, 1, chunk_tokens),
        ((0, 0), (0, 0), (0, hidden_width - chunk_tokens)),
    )
    side_rows = jnp.concatenate([fold_rows, direct_rows], axis=1)
    side_high = side_rows.astype(jnp.bfloat16)
    side_low = (side_rows - side_high.astype(jnp.float32)).astype(jnp.bfloat16)
    combined = jnp.concatenate(
        [
            partial_value.astype(jnp.bfloat16).reshape(tp_count, chunk_tokens, hidden_width),
            side_high,
            side_low,
        ],
        axis=1,
    )
    chunks = lax.all_to_all(combined, "tp", 0, 0, tiled=True)
    mine = jnp.sum(chunks.astype(jnp.float32), axis=0)
    preact = mine[:chunk_tokens]
    head_fold = mine[chunk_tokens] + mine[chunk_tokens + 2]
    direct = mine[chunk_tokens + 1, :chunk_tokens] + mine[chunk_tokens + 3, :chunk_tokens]
    activation = jax.nn.silu(preact).astype(jnp.bfloat16)
    branch = jnp.sum(activation.astype(jnp.float32) * head_fold[None, :], axis=1)
    leading = (lax.axis_index("dp") == 0).astype(jnp.float32)
    own_terms = branch + leading * direct
    picker = (jnp.arange(role_count, dtype=jnp.int32) == lax.axis_index("role")).astype(jnp.float32)
    row_groups = lax.axis_size(("role", "dp"))
    pieces = lax.all_to_all(
        jnp.broadcast_to(own_terms[None, :], (row_groups, chunk_tokens)),
        ("role", "dp"), 0, 0, tiled=True,
    )
    scores = jnp.sum(pieces.reshape(role_count, row_groups // role_count, chunk_tokens), axis=1)
    chunk_rows = chunk_tokens // seq_len
    first_row = lax.axis_index("tp") * chunk_rows
    own_lengths = lax.dynamic_slice_in_dim(lengths, first_row, chunk_rows)
    own_old = lax.dynamic_slice_in_dim(old_log_prob, first_row, chunk_rows)
    slopes, own_advantage = jax.grad(objective, has_aux=True)(scores, own_lengths, own_old)
    own_slope = jnp.sum(slopes * picker[:, None], axis=0)
    sigmoid_value = jax.nn.sigmoid(preact)
    own_grad_pre = (
        own_slope[:, None] * head_fold[None, :] * sigmoid_value * (1.0 + preact * (1.0 - sigmoid_value))
    ).astype(jnp.bfloat16)
    side = jnp.stack([own_slope, own_advantage.reshape(chunk_tokens)])
    side_high = side.astype(jnp.bfloat16)
    side_low = (side - side_high.astype(jnp.float32)).astype(jnp.bfloat16)
    side_rows = jnp.pad(
        jnp.concatenate([side_high, side_low]), ((0, 0), (0, hidden_width - chunk_tokens))
    )
    payload = jnp.concatenate([own_grad_pre, side_rows], axis=0)
    spread = lax.all_to_all(
        jnp.broadcast_to(payload[None], (tp_count,) + payload.shape), "tp", 0, 0, tiled=True
    )
    grad_pre = spread[:, :chunk_tokens].reshape(token_count, hidden_width)
    side_all = (
        spread[:, chunk_tokens : chunk_tokens + 2, :chunk_tokens].astype(jnp.float32)
        + spread[:, chunk_tokens + 2 : chunk_tokens + 4, :chunk_tokens].astype(jnp.float32)
    )
    cotangent = side_all[:, 0].reshape(token_count)
    advantage = side_all[:, 1].reshape(lengths.shape[0], seq_len)
    upstream = (cotangent[:, None] * head_block[None, :]).astype(jnp.bfloat16)
    local = lax.dot_general(
        grad_pre, up_block, (((1,), (1,)), ((), ())), preferred_element_type=jnp.float32
    )
    contrib = (local + leading * upstream.astype(jnp.float32)).astype(jnp.bfloat16)
    received = lax.all_to_all(
        contrib.reshape(role_count, -1, feature_width), "role", 0, 0, tiled=True
    )
    received = jnp.sum(received.astype(jnp.float32), axis=0).astype(jnp.bfloat16)
    received = lax.all_to_all(
        received.reshape(row_groups // role_count, -1), "dp", 0, 0, tiled=True
    )
    summed = jnp.sum(received.astype(jnp.float32), axis=0)
    return (advantage, summed.astype(jnp.bfloat16).reshape(shard_rows, seq_len, feature_width))


def solution(mesh):
    placed = (
        P(("role", "dp"), None, "tp"),
        P(),
        P(),
        P("role", "tp", "dp"),
        P("role", "dp", "tp"),
        P("role", "tp"),
    )
    return jax.shard_map(
        per_device,
        mesh=mesh,
        in_specs=placed,
        out_specs=(P(), P(("role", "dp"), None, "tp")),
        check_vma=False,
    )
```

```python
import jax
import jax.numpy as jnp
from jax import lax
from jax.sharding import PartitionSpec as P

penalty_beta = 0.05
trace_lambda = 0.95
value_weight = 0.5
kl_weight = 0.1
loss_scale = 64.0


def decay_table(seq_len):
    positions = jnp.arange(seq_len, dtype=jnp.int32)
    steps_ahead = positions[None, :] - positions[:, None]
    weights = jnp.power(jnp.float32(trace_lambda), jnp.maximum(steps_ahead, 0).astype(jnp.float32))
    return jnp.where(steps_ahead >= 0, weights, jnp.float32(0.0))


def objective(scores, lengths, old_log_prob):
    row_count, seq_len = old_log_prob.shape
    positions = jnp.arange(seq_len, dtype=jnp.int32)
    live_mask = (positions[None, :] < lengths[:, None]).astype(jnp.float32)
    final_pos = (positions[None, :] == lengths[:, None] - 1).astype(jnp.float32)
    score_grid = scores.reshape(scores.shape[0], row_count, seq_len)
    log_prob = jax.nn.log_sigmoid(score_grid[0])
    ref_log_prob = jax.nn.log_sigmoid(score_grid[1])
    value_est = score_grid[3]
    outcome = jnp.sum(score_grid[2] * final_pos, axis=1, keepdims=True)
    token_gain = live_mask * -penalty_beta * (log_prob - ref_log_prob) + final_pos * outcome
    frozen = live_mask * value_est
    next_value = jnp.concatenate([frozen[:, 1:], jnp.zeros((row_count, 1), jnp.float32)], axis=1)
    step_error = lax.stop_gradient(token_gain + next_value - frozen)
    advantage = live_mask * jnp.dot(
        step_error, decay_table(seq_len).T, precision=lax.Precision.HIGHEST
    )
    prob_ratio = jnp.exp(log_prob - old_log_prob)
    target = advantage + lax.stop_gradient(value_est)
    spread = ref_log_prob - log_prob
    per_token = (
        -prob_ratio * advantage
        + value_weight * 0.5 * (value_est - target) ** 2
        + kl_weight * (jnp.exp(spread) - spread - 1.0)
    )
    return (loss_scale * jnp.sum(live_mask * per_token), advantage)


def per_device(states, lengths, old_log_prob, up_weight, down_weight, score_head):
    shard_rows, seq_len, feature_width = states.shape
    up_block = up_weight[0]
    down_block = down_weight[0]
    head_block = score_head[0]
    hidden_width = up_block.shape[1]
    role_count = lax.axis_size("role")
    tp_count = lax.axis_size("tp")
    own_rows = states.reshape(-1, feature_width)
    stage = lax.all_to_all(
        jnp.broadcast_to(own_rows[None], (lax.axis_size("dp"),) + own_rows.shape), "dp", 0, 0, tiled=True
    ).reshape(-1, feature_width)
    dp_count = lax.axis_size("dp")
    core = lax.axis_index("dp") % 2
    halves = stage.reshape(2, -1, feature_width)
    own_half = lax.dynamic_index_in_dim(halves, core, 0, keepdims=False)
    got = lax.all_to_all(
        jnp.broadcast_to(own_half[None], (role_count,) + own_half.shape), "role", 0, 0, tiled=True
    )
    other = lax.ppermute(got, "dp", [(i, i ^ 1) for i in range(dp_count)])
    def project(half):
        flat = half.reshape(-1, feature_width)
        value = jnp.dot(flat, up_block, preferred_element_type=jnp.float32)
        direct_value = jnp.sum(flat.astype(jnp.float32) * head_block[None, :], axis=1)
        return value.reshape(role_count, -1, hidden_width), direct_value.reshape(role_count, -1)

    got_value, got_direct = project(got)
    other_value, other_direct = project(other)

    def in_order(mine_part, partner_part):
        return jnp.where(
            core == 0,
            jnp.concatenate([mine_part, partner_part], axis=1),
            jnp.concatenate([partner_part, mine_part], axis=1),
        )

    partial_value = in_order(got_value, other_value).reshape(-1, hidden_width)
    direct_part = in_order(got_direct, other_direct).reshape(-1)
    token_count = partial_value.shape[0]
    fold_part = jnp.sum(down_block.astype(jnp.float32) * head_block[None, :], axis=1)
    chunk_tokens = token_count // tp_count
    fold_rows = jnp.broadcast_to(fold_part[None, None, :], (tp_count, 1, hidden_width))
    direct_rows = jnp.pad(
        direct_part.reshape(tp_count, 1, chunk_tokens),
        ((0, 0), (0, 0), (0, hidden_width - chunk_tokens)),
    )
    side_rows = jnp.concatenate([fold_rows, direct_rows], axis=1)
    side_high = side_rows.astype(jnp.bfloat16)
    side_low = (side_rows - side_high.astype(jnp.float32)).astype(jnp.bfloat16)
    combined = jnp.concatenate(
        [
            partial_value.astype(jnp.bfloat16).reshape(tp_count, chunk_tokens, hidden_width),
            side_high,
            side_low,
        ],
        axis=1,
    )
    chunks = lax.all_to_all(combined, "tp", 0, 0, tiled=True)
    mine = jnp.sum(chunks.astype(jnp.float32), axis=0)
    preact = mine[:chunk_tokens]
    head_fold = mine[chunk_tokens] + mine[chunk_tokens + 2]
    direct = mine[chunk_tokens + 1, :chunk_tokens] + mine[chunk_tokens + 3, :chunk_tokens]
    activation = jax.nn.silu(preact).astype(jnp.bfloat16)
    branch = jnp.sum(activation.astype(jnp.float32) * head_fold[None, :], axis=1)
    leading = (lax.axis_index("dp") == 0).astype(jnp.float32)
    own_terms = branch + leading * direct
    picker = (jnp.arange(role_count, dtype=jnp.int32) == lax.axis_index("role")).astype(jnp.float32)
    row_groups = lax.axis_size(("role", "dp"))
    pieces = lax.all_to_all(
        jnp.broadcast_to(own_terms[None, :], (row_groups, chunk_tokens)),
        ("role", "dp"), 0, 0, tiled=True,
    )
    scores = jnp.sum(pieces.reshape(role_count, row_groups // role_count, chunk_tokens), axis=1)
    chunk_rows = chunk_tokens // seq_len
    first_row = lax.axis_index("tp") * chunk_rows
    own_lengths = lax.dynamic_slice_in_dim(lengths, first_row, chunk_rows)
    own_old = lax.dynamic_slice_in_dim(old_log_prob, first_row, chunk_rows)
    slopes, own_advantage = jax.grad(objective, has_aux=True)(scores, own_lengths, own_old)
    own_slope = jnp.sum(slopes * picker[:, None], axis=0)
    sigmoid_value = jax.nn.sigmoid(preact)
    own_grad_pre = (
        own_slope[:, None] * head_fold[None, :] * sigmoid_value * (1.0 + preact * (1.0 - sigmoid_value))
    ).astype(jnp.bfloat16)
    side = jnp.stack([own_slope, own_advantage.reshape(chunk_tokens)])
    side_high = side.astype(jnp.bfloat16)
    side_low = (side - side_high.astype(jnp.float32)).astype(jnp.bfloat16)
    side_rows = jnp.pad(
        jnp.concatenate([side_high, side_low]), ((0, 0), (0, hidden_width - chunk_tokens))
    )
    payload = jnp.concatenate([own_grad_pre, side_rows], axis=0)
    spread = lax.all_to_all(
        jnp.broadcast_to(payload[None], (tp_count,) + payload.shape), "tp", 0, 0, tiled=True
    )
    grad_pre = spread[:, :chunk_tokens].reshape(token_count, hidden_width)
    side_all = (
        spread[:, chunk_tokens : chunk_tokens + 2, :chunk_tokens].astype(jnp.float32)
        + spread[:, chunk_tokens + 2 : chunk_tokens + 4, :chunk_tokens].astype(jnp.float32)
    )
    cotangent = side_all[:, 0].reshape(token_count)
    advantage = side_all[:, 1].reshape(lengths.shape[0], seq_len)
    upstream = (cotangent[:, None] * head_block[None, :]).astype(jnp.bfloat16)
    local = lax.dot_general(
        grad_pre, up_block, (((1,), (1,)), ((), ())), preferred_element_type=jnp.float32
    )
    contrib = (local + leading * upstream.astype(jnp.float32)).astype(jnp.bfloat16)
    received = lax.all_to_all(
        contrib.reshape(role_count, -1, feature_width), "role", 0, 0, tiled=True
    )
    received = jnp.sum(received.astype(jnp.float32), axis=0).astype(jnp.bfloat16)
    received = lax.all_to_all(
        received.reshape(row_groups // role_count, -1), "dp", 0, 0, tiled=True
    )
    summed = jnp.sum(received.astype(jnp.float32), axis=0)
    return (advantage, summed.astype(jnp.bfloat16).reshape(shard_rows, seq_len, feature_width))


def solution(mesh):
    placed = (
        P(("role", "dp"), None, "tp"),
        P(),
        P(),
        P("role", "tp", "dp"),
        P("role", "dp", "tp"),
        P("role", "tp"),
    )
    return jax.shard_map(
        per_device,
        mesh=mesh,
        in_specs=placed,
        out_specs=(P(), P(("role", "dp"), None, "tp")),
        check_vma=False,
    )
```

```python
import jax
import jax.numpy as jnp
from jax import lax
from jax.sharding import PartitionSpec as P

penalty_beta = 0.05
trace_lambda = 0.95
value_weight = 0.5
kl_weight = 0.1
loss_scale = 64.0


def decay_table(seq_len):
    positions = jnp.arange(seq_len, dtype=jnp.int32)
    steps_ahead = positions[None, :] - positions[:, None]
    weights = jnp.power(jnp.float32(trace_lambda), jnp.maximum(steps_ahead, 0).astype(jnp.float32))
    return jnp.where(steps_ahead >= 0, weights, jnp.float32(0.0))


def objective(scores, lengths, old_log_prob):
    row_count, seq_len = old_log_prob.shape
    positions = jnp.arange(seq_len, dtype=jnp.int32)
    live_mask = (positions[None, :] < lengths[:, None]).astype(jnp.float32)
    final_pos = (positions[None, :] == lengths[:, None] - 1).astype(jnp.float32)
    score_grid = scores.reshape(scores.shape[0], row_count, seq_len)
    log_prob = jax.nn.log_sigmoid(score_grid[0])
    ref_log_prob = jax.nn.log_sigmoid(score_grid[1])
    value_est = score_grid[3]
    outcome = jnp.sum(score_grid[2] * final_pos, axis=1, keepdims=True)
    token_gain = live_mask * -penalty_beta * (log_prob - ref_log_prob) + final_pos * outcome
    frozen = live_mask * value_est
    next_value = jnp.concatenate([frozen[:, 1:], jnp.zeros((row_count, 1), jnp.float32)], axis=1)
    step_error = lax.stop_gradient(token_gain + next_value - frozen)
    advantage = live_mask * jnp.dot(
        step_error, decay_table(seq_len).T, precision=lax.Precision.HIGHEST
    )
    prob_ratio = jnp.exp(log_prob - old_log_prob)
    target = advantage + lax.stop_gradient(value_est)
    spread = ref_log_prob - log_prob
    per_token = (
        -prob_ratio * advantage
        + value_weight * 0.5 * (value_est - target) ** 2
        + kl_weight * (jnp.exp(spread) - spread - 1.0)
    )
    return (loss_scale * jnp.sum(live_mask * per_token), advantage)


def per_device(states, lengths, old_log_prob, up_weight, down_weight, score_head):
    shard_rows, seq_len, feature_width = states.shape
    up_block = up_weight[0]
    down_block = down_weight[0]
    head_block = score_head[0]
    hidden_width = up_block.shape[1]
    role_count = lax.axis_size("role")
    tp_count = lax.axis_size("tp")
    stage = lax.all_gather(states, "dp", axis=0, tiled=True).reshape(-1, feature_width)
    dp_count = lax.axis_size("dp")
    core = lax.axis_index("dp") % 2
    halves = stage.reshape(2, -1, feature_width)
    own_half = lax.dynamic_index_in_dim(halves, core, 0, keepdims=False)
    got = lax.all_to_all(
        jnp.broadcast_to(own_half[None], (role_count,) + own_half.shape), "role", 0, 0, tiled=True
    )
    other = lax.ppermute(got, "dp", [(i, i ^ 1) for i in range(dp_count)])
    def project(half):
        flat = half.reshape(-1, feature_width)
        value = jnp.dot(flat, up_block, preferred_element_type=jnp.float32)
        direct_value = jnp.sum(flat.astype(jnp.float32) * head_block[None, :], axis=1)
        return value.reshape(role_count, -1, hidden_width), direct_value.reshape(role_count, -1)

    got_value, got_direct = project(got)
    other_value, other_direct = project(other)

    def in_order(mine_part, partner_part):
        return jnp.where(
            core == 0,
            jnp.concatenate([mine_part, partner_part], axis=1),
            jnp.concatenate([partner_part, mine_part], axis=1),
        )

    partial_value = in_order(got_value, other_value).reshape(-1, hidden_width)
    direct_part = in_order(got_direct, other_direct).reshape(-1)
    token_count = partial_value.shape[0]
    fold_part = jnp.sum(down_block.astype(jnp.float32) * head_block[None, :], axis=1)
    chunk_tokens = token_count // tp_count
    fold_rows = jnp.broadcast_to(fold_part[None, None, :], (tp_count, 1, hidden_width))
    direct_rows = jnp.pad(
        direct_part.reshape(tp_count, 1, chunk_tokens),
        ((0, 0), (0, 0), (0, hidden_width - chunk_tokens)),
    )
    side_rows = jnp.concatenate([fold_rows, direct_rows], axis=1)
    side_high = side_rows.astype(jnp.bfloat16)
    side_low = (side_rows - side_high.astype(jnp.float32)).astype(jnp.bfloat16)
    combined = jnp.concatenate(
        [
            partial_value.astype(jnp.bfloat16).reshape(tp_count, chunk_tokens, hidden_width),
            side_high,
            side_low,
        ],
        axis=1,
    )
    chunks = lax.all_to_all(combined, "tp", 0, 0, tiled=True)
    mine = jnp.sum(chunks.astype(jnp.float32), axis=0)
    preact = mine[:chunk_tokens]
    head_fold = mine[chunk_tokens] + mine[chunk_tokens + 2]
    direct = mine[chunk_tokens + 1, :chunk_tokens] + mine[chunk_tokens + 3, :chunk_tokens]
    activation = jax.nn.silu(preact).astype(jnp.bfloat16)
    branch = jnp.sum(activation.astype(jnp.float32) * head_fold[None, :], axis=1)
    leading = (lax.axis_index("dp") == 0).astype(jnp.float32)
    own_terms = branch + leading * direct
    picker = (jnp.arange(role_count, dtype=jnp.int32) == lax.axis_index("role")).astype(jnp.float32)
    row_groups = lax.axis_size(("role", "dp"))
    pieces = lax.all_to_all(
        jnp.broadcast_to(own_terms[None, :], (row_groups, chunk_tokens)),
        ("role", "dp"), 0, 0, tiled=True,
    )
    scores = jnp.sum(pieces.reshape(role_count, row_groups // role_count, chunk_tokens), axis=1)
    chunk_rows = chunk_tokens // seq_len
    first_row = lax.axis_index("tp") * chunk_rows
    own_lengths = lax.dynamic_slice_in_dim(lengths, first_row, chunk_rows)
    own_old = lax.dynamic_slice_in_dim(old_log_prob, first_row, chunk_rows)
    slopes, own_advantage = jax.grad(objective, has_aux=True)(scores, own_lengths, own_old)
    own_slope = jnp.sum(slopes * picker[:, None], axis=0)
    sigmoid_value = jax.nn.sigmoid(preact)
    own_grad_pre = (
        own_slope[:, None] * head_fold[None, :] * sigmoid_value * (1.0 + preact * (1.0 - sigmoid_value))
    ).astype(jnp.bfloat16)
    side = jnp.stack([own_slope, own_advantage.reshape(chunk_tokens)])
    side_high = side.astype(jnp.bfloat16)
    side_low = (side - side_high.astype(jnp.float32)).astype(jnp.bfloat16)
    side_rows = jnp.pad(
        jnp.concatenate([side_high, side_low]), ((0, 0), (0, hidden_width - chunk_tokens))
    )
    payload = jnp.concatenate([own_grad_pre, side_rows], axis=0)
    spread = lax.all_to_all(
        jnp.broadcast_to(payload[None], (tp_count,) + payload.shape), "tp", 0, 0, tiled=True
    )
    grad_pre = spread[:, :chunk_tokens].reshape(token_count, hidden_width)
    side_all = (
        spread[:, chunk_tokens : chunk_tokens + 2, :chunk_tokens].astype(jnp.float32)
        + spread[:, chunk_tokens + 2 : chunk_tokens + 4, :chunk_tokens].astype(jnp.float32)
    )
    cotangent = side_all[:, 0].reshape(token_count)
    advantage = side_all[:, 1].reshape(lengths.shape[0], seq_len)
    upstream = (cotangent[:, None] * head_block[None, :]).astype(jnp.bfloat16)
    local = lax.dot_general(
        grad_pre, up_block, (((1,), (1,)), ((), ())), preferred_element_type=jnp.float32
    )
    contrib = (local + leading * upstream.astype(jnp.float32)).astype(jnp.bfloat16)
    received = lax.all_to_all(
        contrib.reshape(role_count, -1, feature_width), "role", 0, 0, tiled=True
    )
    received = jnp.sum(received.astype(jnp.float32), axis=0).astype(jnp.bfloat16)
    received = lax.all_to_all(
        received.reshape(row_groups // role_count, -1), "dp", 0, 0, tiled=True
    )
    summed = jnp.sum(received.astype(jnp.float32), axis=0)
    return (advantage, summed.astype(jnp.bfloat16).reshape(shard_rows, seq_len, feature_width))


def solution(mesh):
    placed = (
        P(("role", "dp"), None, "tp"),
        P(),
        P(),
        P("role", "tp", "dp"),
        P("role", "dp", "tp"),
        P("role", "tp"),
    )
    return jax.shard_map(
        per_device,
        mesh=mesh,
        in_specs=placed,
        out_specs=(P(), P(("role", "dp"), None, "tp")),
        check_vma=False,
    )
```

```python
import jax
import jax.numpy as jnp
from jax import lax
from jax.sharding import PartitionSpec as P

penalty_beta = 0.05
trace_lambda = 0.95
value_weight = 0.5
kl_weight = 0.1
loss_scale = 64.0


def decay_table(seq_len):
    positions = jnp.arange(seq_len, dtype=jnp.int32)
    steps_ahead = positions[None, :] - positions[:, None]
    weights = jnp.power(jnp.float32(trace_lambda), jnp.maximum(steps_ahead, 0).astype(jnp.float32))
    return jnp.where(steps_ahead >= 0, weights, jnp.float32(0.0))


def objective(scores, lengths, old_log_prob):
    row_count, seq_len = old_log_prob.shape
    positions = jnp.arange(seq_len, dtype=jnp.int32)
    live_mask = (positions[None, :] < lengths[:, None]).astype(jnp.float32)
    final_pos = (positions[None, :] == lengths[:, None] - 1).astype(jnp.float32)
    score_grid = scores.reshape(scores.shape[0], row_count, seq_len)
    log_prob = jax.nn.log_sigmoid(score_grid[0])
    ref_log_prob = jax.nn.log_sigmoid(score_grid[1])
    value_est = score_grid[3]
    outcome = jnp.sum(score_grid[2] * final_pos, axis=1, keepdims=True)
    token_gain = live_mask * -penalty_beta * (log_prob - ref_log_prob) + final_pos * outcome
    frozen = live_mask * value_est
    next_value = jnp.concatenate([frozen[:, 1:], jnp.zeros((row_count, 1), jnp.float32)], axis=1)
    step_error = lax.stop_gradient(token_gain + next_value - frozen)
    advantage = live_mask * jnp.dot(
        step_error, decay_table(seq_len).T, precision=lax.Precision.HIGHEST
    )
    prob_ratio = jnp.exp(log_prob - old_log_prob)
    target = advantage + lax.stop_gradient(value_est)
    spread = ref_log_prob - log_prob
    per_token = (
        -prob_ratio * advantage
        + value_weight * 0.5 * (value_est - target) ** 2
        + kl_weight * (jnp.exp(spread) - spread - 1.0)
    )
    return (loss_scale * jnp.sum(live_mask * per_token), advantage)


def per_device(states, lengths, old_log_prob, up_weight, down_weight, score_head):
    shard_rows, seq_len, feature_width = states.shape
    up_block = up_weight[0]
    down_block = down_weight[0]
    head_block = score_head[0]
    hidden_width = up_block.shape[1]
    role_count = lax.axis_size("role")
    tp_count = lax.axis_size("tp")
    stage = lax.all_gather(states, "dp", axis=0, tiled=True).reshape(-1, feature_width)
    dp_count = lax.axis_size("dp")
    core = lax.axis_index("dp") % 2
    halves = stage.reshape(2, -1, feature_width)
    own_half = lax.dynamic_index_in_dim(halves, core, 0, keepdims=False)
    got = lax.all_to_all(
        jnp.broadcast_to(own_half[None], (role_count,) + own_half.shape), "role", 0, 0, tiled=True
    )
    other = lax.ppermute(got, "dp", [(i, i ^ 1) for i in range(dp_count)])
    def project(half):
        flat = half.reshape(-1, feature_width)
        value = jnp.dot(flat, up_block, preferred_element_type=jnp.float32)
        direct_value = jnp.sum(flat.astype(jnp.float32) * head_block[None, :], axis=1)
        return value.reshape(role_count, -1, hidden_width), direct_value.reshape(role_count, -1)

    got_value, got_direct = project(got)
    other_value, other_direct = project(other)

    def in_order(mine_part, partner_part):
        return jnp.where(
            core == 0,
            jnp.concatenate([mine_part, partner_part], axis=1),
            jnp.concatenate([partner_part, mine_part], axis=1),
        )

    partial_value = in_order(got_value, other_value).reshape(-1, hidden_width)
    direct_part = in_order(got_direct, other_direct).reshape(-1)
    token_count = partial_value.shape[0]
    fold_part = jnp.dot(
        down_block.astype(jnp.float32), head_block, precision=lax.Precision.HIGHEST
    )
    chunk_tokens = token_count // tp_count
    fold_rows = jnp.broadcast_to(fold_part[None, None, :], (tp_count, 1, hidden_width))
    direct_rows = jnp.pad(
        direct_part.reshape(tp_count, 1, chunk_tokens),
        ((0, 0), (0, 0), (0, hidden_width - chunk_tokens)),
    )
    side_rows = jnp.concatenate([fold_rows, direct_rows], axis=1)
    side_high = side_rows.astype(jnp.bfloat16)
    side_low = (side_rows - side_high.astype(jnp.float32)).astype(jnp.bfloat16)
    combined = jnp.concatenate(
        [
            partial_value.astype(jnp.bfloat16).reshape(tp_count, chunk_tokens, hidden_width),
            side_high,
            side_low,
        ],
        axis=1,
    )
    chunks = lax.all_to_all(combined, "tp", 0, 0, tiled=True)
    mine = jnp.sum(chunks.astype(jnp.float32), axis=0)
    preact = mine[:chunk_tokens]
    head_fold = mine[chunk_tokens] + mine[chunk_tokens + 2]
    direct = mine[chunk_tokens + 1, :chunk_tokens] + mine[chunk_tokens + 3, :chunk_tokens]
    activation = jax.nn.silu(preact).astype(jnp.bfloat16)
    branch = jnp.sum(activation.astype(jnp.float32) * head_fold[None, :], axis=1)
    leading = (lax.axis_index("dp") == 0).astype(jnp.float32)
    own_terms = branch + leading * direct
    picker = (jnp.arange(role_count, dtype=jnp.int32) == lax.axis_index("role")).astype(jnp.float32)
    row_groups = lax.axis_size(("role", "dp"))
    pieces = lax.all_to_all(
        jnp.broadcast_to(own_terms[None, :], (row_groups, chunk_tokens)),
        ("role", "dp"), 0, 0, tiled=True,
    )
    scores = jnp.sum(pieces.reshape(role_count, row_groups // role_count, chunk_tokens), axis=1)
    chunk_rows = chunk_tokens // seq_len
    first_row = lax.axis_index("tp") * chunk_rows
    own_lengths = lax.dynamic_slice_in_dim(lengths, first_row, chunk_rows)
    own_old = lax.dynamic_slice_in_dim(old_log_prob, first_row, chunk_rows)
    slopes, own_advantage = jax.grad(objective, has_aux=True)(scores, own_lengths, own_old)
    own_slope = jnp.sum(slopes * picker[:, None], axis=0)
    sigmoid_value = jax.nn.sigmoid(preact)
    own_grad_pre = (
        own_slope[:, None] * head_fold[None, :] * sigmoid_value * (1.0 + preact * (1.0 - sigmoid_value))
    ).astype(jnp.bfloat16)
    side = jnp.stack([own_slope, own_advantage.reshape(chunk_tokens)])
    side_high = side.astype(jnp.bfloat16)
    side_low = (side - side_high.astype(jnp.float32)).astype(jnp.bfloat16)
    side_rows = jnp.pad(
        jnp.concatenate([side_high, side_low]), ((0, 0), (0, hidden_width - chunk_tokens))
    )
    payload = jnp.concatenate([own_grad_pre, side_rows], axis=0)
    spread = lax.all_to_all(
        jnp.broadcast_to(payload[None], (tp_count,) + payload.shape), "tp", 0, 0, tiled=True
    )
    grad_pre = spread[:, :chunk_tokens].reshape(token_count, hidden_width)
    side_all = (
        spread[:, chunk_tokens : chunk_tokens + 2, :chunk_tokens].astype(jnp.float32)
        + spread[:, chunk_tokens + 2 : chunk_tokens + 4, :chunk_tokens].astype(jnp.float32)
    )
    cotangent = side_all[:, 0].reshape(token_count)
    advantage = side_all[:, 1].reshape(lengths.shape[0], seq_len)
    upstream = (cotangent[:, None] * head_block[None, :]).astype(jnp.bfloat16)
    local = lax.dot_general(
        grad_pre, up_block, (((1,), (1,)), ((), ())), preferred_element_type=jnp.float32
    )
    contrib = (local + leading * upstream.astype(jnp.float32)).astype(jnp.bfloat16)
    received = lax.all_to_all(
        contrib.reshape(role_count, -1, feature_width), "role", 0, 0, tiled=True
    )
    received = jnp.sum(received.astype(jnp.float32), axis=0).astype(jnp.bfloat16)
    received = lax.all_to_all(
        received.reshape(row_groups // role_count, -1), "dp", 0, 0, tiled=True
    )
    summed = jnp.sum(received.astype(jnp.float32), axis=0)
    return (advantage, summed.astype(jnp.bfloat16).reshape(shard_rows, seq_len, feature_width))


def solution(mesh):
    placed = (
        P(("role", "dp"), None, "tp"),
        P(),
        P(),
        P("role", "tp", "dp"),
        P("role", "dp", "tp"),
        P("role", "tp"),
    )
    return jax.shard_map(
        per_device,
        mesh=mesh,
        in_specs=placed,
        out_specs=(P(), P(("role", "dp"), None, "tp")),
        check_vma=False,
    )
```
